512 devices in a mesh: ctx: 64 (over z, y_lo, core), head: 8 (over y_hi, x).
Axes of the slice: x: 4, y: 4 (y_hi: 2, y_lo: 2; y = y_hi * 2 + y_lo), z: 16, core: 2. Of those that a mesh axis runs over, the one named last changes fastest.
Arguments:
- events: bfloat16 [16384, 1024], P('ctx'), may hold values from -16 to 16
- ssm_input: bfloat16 [16384, 2048], P('ctx', 'head'), may hold values from -1.5 to 1.5
- gate_input: bfloat16 [16384, 2048], P('ctx', 'head'), may hold values from -6 to 6
- grad_out: bfloat16 [16384, 2048], P('ctx', 'head'), may hold values from -0.015625 to 0.015625
- shared_b: bfloat16 [16384, 128], P('ctx'), may hold values from -6 to 6
- shared_c: bfloat16 [16384, 128], P('ctx'), may hold values from -6 to 6
- log_decay: float32 [32, 16384], P('head', 'ctx'), may hold values from -1 to 0, as said below
- entry_state: float32 [64, 32, 128, 64], P('ctx', 'head'), may hold values from -48 to 48
- w_gate: bfloat16 [1024, 2048], P(None, 'head'), may hold values from -0.1875 to 0.1875
- w_value: bfloat16 [1024, 2048], P(None, 'head'), may hold values from -0.1875 to 0.1875
- w_shared: bfloat16 [1024, 256], P(None, 'head'), may hold values from -0.1875 to 0.1875
Outputs:
- grad_input: bfloat16 [16384, 1024], P('ctx', 'head')
- grad_w_gate: float32 [1024, 2048], P('ctx', 'head')
- grad_w_value: float32 [1024, 2048], P('ctx', 'head')
- grad_w_shared: float32 [1024, 256], P('ctx', 'head')
The draws below stay inside these ranges and needn't reach their ends.
Inputs may be any that keep to these rules, and one draw needn't show every extreme that they name: `log_decay`: every entry is negative.
All inputs are finite; a program needn't handle non-finite values.
Results may differ from the reference program's by a relative error of at most 0.015.
Values may be sent and summed in bfloat16 or wider, within the bound.
No kernel may reach another device: no remote copies, remote signals or barrier semaphores. Data moves between devices by JAX's collectives and lax.ppermute only.
A program may use at most 64 MiB of HBM per device.

```python
import math
import jax
import jax.numpy as jnp
from jax import lax

D = 1024
HEAD_TOTAL = 32
HEAD_DIM = 64
STATE = 128
SPAN = 256
L_DEV = 256
TOKEN_COUNT = 16384
BLOCKS = 64
GROUP_HEADS = 4
N_HEAD = 8


def draw_log_decay(key, part):
    random_subkeys = jax.random.split(key, 7)
    fast_share = 5
    fast_heads = jax.random.randint(random_subkeys[0], (HEAD_TOTAL,), 0, 10) < fast_share
    fast_rates = jnp.exp(jax.random.uniform(random_subkeys[1], (HEAD_TOTAL,), jnp.float32, math.log(1.0 / 50.0), math.log(1.0 / 30.0)))
    slow_rates = 0.12 * math.log(10.0) / TOKEN_COUNT * jax.random.uniform(random_subkeys[2], (HEAD_TOTAL,), jnp.float32, 0.5, 1.0)
    head_rates = jnp.where(fast_heads, fast_rates, slow_rates)
    blocks = TOKEN_COUNT // L_DEV
    block_factor = jnp.exp(jax.random.uniform(random_subkeys[3], (HEAD_TOTAL, blocks, 1), jnp.float32, math.log(0.5), math.log(2.0)))
    event_factor = jax.random.uniform(random_subkeys[4], (HEAD_TOTAL, blocks, L_DEV), jnp.float32, 0.5, 1.5)
    forget_rates = -(head_rates[:, None, None] * block_factor * event_factor).reshape(HEAD_TOTAL, TOKEN_COUNT)
    spike_position = jax.random.randint(random_subkeys[5], (HEAD_TOTAL, 2), 0, TOKEN_COUNT)
    spike_penalty = jax.random.uniform(random_subkeys[6], (HEAD_TOTAL, 2), jnp.float32, math.log(0.5), math.log(0.8))
    spike_matches = jnp.arange(TOKEN_COUNT, dtype=jnp.int32)[None, None, :] == spike_position[:, :, None]
    event_spikes = jnp.sum(jnp.where(spike_matches, spike_penalty[:, :, None], 0.0), axis=1)
    return (forget_rates + event_spikes).astype(jnp.float32)


def strengthened(values, stream_key, source, target, blocks, factor):
    def block_of(axis_at):
        return (jnp.arange(values.shape[axis_at]) // (values.shape[axis_at] // blocks)).reshape((-1,) + (1,) * (values.ndim - 1 - axis_at))

    one_side = jax.random.permutation(stream_key, blocks)[block_of(target)]
    second = (block_of(target) + blocks // 2) % blocks
    return jnp.where((block_of(source) == one_side) | (block_of(source) == second), factor * values, values)


def levels(rng, extent, pieces, low, top_value):
    gain, own = 1.0, jax.random.fold_in(rng, 6)
    for axis_at, shards_of in pieces:
        steps = jnp.exp(jax.random.uniform(jax.random.fold_in(own, axis_at), (shards_of,), jnp.float32, low / len(pieces), top_value / len(pieces)))
        gain = gain * jnp.repeat(steps, extent[axis_at] // shards_of).reshape([-1 if axis == axis_at else 1 for axis in range(len(extent))])
    return gain


def scatter_about(own_key, shape, deviation, bound, shards=(), kind=jnp.bfloat16):
    drawn = jax.random.normal(own_key, shape, jnp.float32) * deviation
    if len(shards) > 0:
        drawn = levels(own_key, shape, shards, -0.22, 0.18) * drawn
    return jnp.clip(drawn, min=-bound, max=bound).astype(kind)


def noise_with(stream_key, extent, scale, reach, cuts, heavy, kind=jnp.bfloat16):
    values = scale * jax.random.normal(stream_key, extent, jnp.float32)
    if cuts:
        values = values * levels(stream_key, extent, cuts, -0.22, 0.18)
    return jnp.clip(strengthened(values, jax.random.fold_in(stream_key, 3), *heavy), -reach, reach).astype(kind)


def setup_inputs(seed: int = 0) -> dict:
    arg_keys = jax.random.split(jax.random.key(seed), 12)
    events = noise_with(arg_keys[0], (TOKEN_COUNT, D), 1.0, 16.0, ((0, 64),), (0, 1, 64, 4.0))
    ssm_input = scatter_about(arg_keys[1], (TOKEN_COUNT, HEAD_TOTAL * HEAD_DIM), 0.25, 1.5, ((0, 64), (1, 8)))
    gate_input = scatter_about(arg_keys[2], (TOKEN_COUNT, HEAD_TOTAL * HEAD_DIM), 1.0, 6.0, ((0, 64), (1, 8)))
    grad_out = scatter_about(arg_keys[3], (TOKEN_COUNT, HEAD_TOTAL * HEAD_DIM), 0.003, 0.015625, ((0, 64), (1, 8)))
    shared_b = scatter_about(arg_keys[4], (TOKEN_COUNT, STATE), 1.0, 6.0, ((0, 64),))
    shared_c = scatter_about(arg_keys[5], (TOKEN_COUNT, STATE), 1.0, 6.0, ((0, 64),))
    log_decay = draw_log_decay(jax.random.fold_in(arg_keys[11], 71), 0)
    entry_state = scatter_about(arg_keys[7], (BLOCKS, HEAD_TOTAL, STATE, HEAD_DIM), 8.0, 48.0, ((0, 64), (1, 8)), jnp.float32)
    w_gate = scatter_about(arg_keys[8], (D, HEAD_TOTAL * HEAD_DIM), D ** -0.5, 0.1875, ((1, 8),))
    w_value = scatter_about(arg_keys[9], (D, HEAD_TOTAL * HEAD_DIM), D ** -0.5, 0.1875, ((1, 8),))
    w_shared = scatter_about(arg_keys[10], (D, 2 * STATE), D ** -0.5, 0.1875, ((1, 8),))
    return dict(events=events, ssm_input=ssm_input, gate_input=gate_input, grad_out=grad_out, shared_b=shared_b, shared_c=shared_c, log_decay=log_decay, entry_state=entry_state, w_gate=w_gate, w_value=w_value, w_shared=w_shared)


highest = lax.Precision.HIGHEST

def ssd_partials(ssm_input, gate_input, grad_out, shared_b, shared_c, log_decay, entry, block_len):
    head_count, length = log_decay.shape
    head_width = ssm_input.shape[1] // head_count
    span_count = length // block_len
    values_f = ssm_input.astype(jnp.float32).reshape(span_count, block_len, head_count, head_width)
    gates_f = gate_input.astype(jnp.float32).reshape(span_count, block_len, head_count, head_width)
    grad_f = grad_out.astype(jnp.float32).reshape(span_count, block_len, head_count, head_width)
    shared_bf = shared_b.astype(jnp.float32).reshape(span_count, block_len, shared_b.shape[1])
    shared_cf = shared_c.astype(jnp.float32).reshape(span_count, block_len, shared_c.shape[1])
    cumlog = jnp.cumsum(log_decay.reshape(head_count, span_count, block_len), axis=2)
    totals = cumlog[:, :, -1]
    causal = jnp.arange(block_len)[:, None] >= jnp.arange(block_len)[None, :]
    spread = cumlog[:, :, :, None] - cumlog[:, :, None, :]
    decay_mat = jnp.where(causal, jnp.exp(jnp.minimum(spread, 0.0)), 0.0)
    scores = jnp.einsum('ktn,ksn->kts', shared_cf, shared_bf, precision=highest)
    weighted = decay_mat * scores[None]
    to_end = jnp.exp(totals[:, :, None] - cumlog).transpose(1, 2, 0)
    from_start = jnp.exp(cumlog).transpose(1, 2, 0)
    scaled_x = values_f * to_end[..., None]
    local_states = jnp.einsum('ksn,kshp->khnp', shared_bf, scaled_x, precision=highest)
    span_decay = jnp.exp(totals).T

    def forward_step(running, inputs):
        decay_k, local_k = inputs
        return (decay_k[:, None, None] * running + local_k, running)
    _, entries = lax.scan(forward_step, entry, (span_decay, local_states))
    ssm_out = jnp.einsum('hkts,kshp->kthp', weighted, values_f, precision=highest)
    ssm_out = ssm_out + from_start[..., None] * jnp.einsum('ktn,khnp->kthp', shared_cf, entries, precision=highest)
    gate_sig = jax.nn.sigmoid(gates_f)
    grad_y = grad_f * gates_f * gate_sig
    grad_z = grad_f * ssm_out * gate_sig * (1.0 + gates_f * (1.0 - gate_sig))
    products = decay_mat * jnp.einsum('kthp,kshp->hkts', grad_y, values_f, precision=highest)
    scaled_dy = grad_y * from_start[..., None]
    grad_c = jnp.einsum('hkts,ksn->ktn', products, shared_bf, precision=highest)
    grad_c = grad_c + jnp.einsum('kthp,khnp->ktn', scaled_dy, entries, precision=highest)
    grad_b = jnp.einsum('hkst,ksn->ktn', products, shared_cf, precision=highest)
    grad_x = jnp.einsum('hkst,kshp->kthp', weighted, grad_y, precision=highest)
    block_terms = jnp.einsum('ksn,kshp->khnp', shared_cf, scaled_dy, precision=highest)

    def backward_step(running, inputs):
        decay_k, term_k = inputs
        return (term_k + decay_k[:, None, None] * running, running)
    block_sum, later_sums = lax.scan(backward_step, jnp.zeros_like(entry), (span_decay, block_terms), reverse=True)
    block_log = lax.optimization_barrier(jnp.sum(totals, axis=1))
    suffix = block_log[None, :] - jnp.cumsum(totals, axis=1).T
    grad_z_out = grad_z.reshape(length, head_count * head_width).astype(jnp.bfloat16)
    return (grad_z_out, grad_x, grad_b, grad_c, later_sums, suffix, to_end, scaled_x, shared_bf, block_sum, block_log)

def finish_block(partials, incoming):
    grad_z_out, grad_x, grad_b, grad_c, later_sums, suffix, to_end, scaled_x, shared_bf, block_sum, block_log = partials
    carried = later_sums + jnp.exp(suffix)[:, :, None, None] * incoming[None]
    grad_x = grad_x + to_end[..., None] * jnp.einsum('ktn,khnp->kthp', shared_bf, carried, precision=highest)
    grad_b = grad_b + jnp.einsum('kthp,khnp->ktn', scaled_x, carried, precision=highest)
    length = grad_z_out.shape[0]
    grad_x_out = grad_x.reshape(length, grad_z_out.shape[1]).astype(jnp.bfloat16)
    grad_bc = jnp.concatenate([grad_b.reshape(length, -1), grad_c.reshape(length, -1)], axis=1)
    return (grad_z_out, grad_x_out, grad_bc)

def reference(events, ssm_input, gate_input, grad_out, shared_b, shared_c, log_decay, entry_state, w_gate, w_value, w_shared):
    blocks = TOKEN_COUNT // L_DEV

    def by_block(array):
        return array.reshape(blocks, L_DEV, array.shape[1])
    decays = log_decay.reshape(HEAD_TOTAL, blocks, L_DEV).transpose(1, 0, 2)

    def block_step(incoming, inputs):
        part_x, part_g, part_o, part_b, part_c, part_d, part_e = inputs
        partials = ssd_partials(part_x, part_g, part_o, part_b, part_c, part_d, part_e, SPAN)
        outputs = finish_block(partials, incoming)
        return (partials[9] + jnp.exp(partials[10])[:, None, None] * incoming, outputs)
    initial = jnp.zeros((HEAD_TOTAL, STATE, HEAD_DIM), jnp.float32)
    stacked = (by_block(ssm_input), by_block(gate_input), by_block(grad_out), by_block(shared_b), by_block(shared_c), decays, entry_state)
    _, (grad_z, grad_x, grad_bc) = lax.scan(block_step, initial, stacked, reverse=True)
    grad_z = grad_z.reshape(TOKEN_COUNT, HEAD_TOTAL * HEAD_DIM)
    grad_x = grad_x.reshape(TOKEN_COUNT, HEAD_TOTAL * HEAD_DIM)
    grad_bc = grad_bc.reshape(TOKEN_COUNT, 2 * STATE).astype(jnp.bfloat16)
    head_cols = GROUP_HEADS * HEAD_DIM
    shared_cols = 2 * STATE // N_HEAD
    summed = jnp.zeros((TOKEN_COUNT, D), jnp.float32)
    for group in range(N_HEAD):
        low_head = group * head_cols
        high_head = low_head + head_cols
        low_shared = group * shared_cols
        high_shared = low_shared + shared_cols
        partial_value = jnp.dot(grad_z[:, low_head:high_head], w_gate[:, low_head:high_head].T, preferred_element_type=jnp.float32)
        partial_value = partial_value + jnp.dot(grad_x[:, low_head:high_head], w_value[:, low_head:high_head].T, preferred_element_type=jnp.float32)
        partial_value = partial_value + jnp.dot(grad_bc[:, low_shared:high_shared], w_shared[:, low_shared:high_shared].T, preferred_element_type=jnp.float32)
        summed = summed + lax.optimization_barrier(partial_value.astype(jnp.bfloat16)).astype(jnp.float32)
    grad_input = summed.astype(jnp.bfloat16)
    norm_scale = 1.0 / math.sqrt(TOKEN_COUNT)
    grad_w_gate = jnp.dot(events.T, grad_z, preferred_element_type=jnp.float32) * norm_scale
    grad_w_value = jnp.dot(events.T, grad_x, preferred_element_type=jnp.float32) * norm_scale
    grad_w_shared = jnp.dot(events.T, grad_bc, preferred_element_type=jnp.float32) * norm_scale
    return (grad_input, grad_w_gate, grad_w_value, grad_w_shared)
```

```python
import math

import jax
import jax.numpy as jnp
from jax import lax
from jax.sharding import PartitionSpec as P

SPAN = 256


highest = lax.Precision.HIGHEST


def suffix_scan(part, axis):
    count = lax.axis_size(axis)
    place = lax.axis_index(axis)

    def shifted(tree, step):
        pairs = [(source, source - step) for source in range(step, count)]
        return jax.tree.map(lambda a: lax.ppermute(a, axis, pairs), tree)

    def combine(near, far):
        return (near[0] * far[0], near[1] + near[0][:, None, None] * far[1])

    state = shifted(part, 1)
    valid = place + 1 < count
    state = (jnp.where(valid, state[0], 1.0), jnp.where(valid, state[1], 0.0))
    step = 1
    while step < count:
        far = shifted(state, step)
        joined = combine(state, far)
        inside = place + step < count
        state = (
            jnp.where(inside, joined[0], state[0]),
            jnp.where(inside, joined[1], state[1]),
        )
        step *= 2
    return state


def ssd_partials(ssm_input, gate_input, grad_out, shared_b, shared_c, log_decay, entry, block_len):
    head_count, length = log_decay.shape
    head_width = ssm_input.shape[1] // head_count
    span_count = length // block_len
    values_f = ssm_input.astype(jnp.float32).reshape(span_count, block_len, head_count, head_width)
    gates_f = gate_input.astype(jnp.float32).reshape(span_count, block_len, head_count, head_width)
    grad_f = grad_out.astype(jnp.float32).reshape(span_count, block_len, head_count, head_width)
    shared_bf = shared_b.astype(jnp.float32).reshape(span_count, block_len, shared_b.shape[1])
    shared_cf = shared_c.astype(jnp.float32).reshape(span_count, block_len, shared_c.shape[1])
    cumlog = jnp.cumsum(log_decay.reshape(head_count, span_count, block_len), axis=2)
    totals = cumlog[:, :, -1]
    causal = jnp.arange(block_len)[:, None] >= jnp.arange(block_len)[None, :]
    spread = cumlog[:, :, :, None] - cumlog[:, :, None, :]
    decay_mat = jnp.where(causal, jnp.exp(jnp.minimum(spread, 0.0)), 0.0)
    shared_c_blocks = shared_c.reshape(span_count, block_len, shared_c.shape[1])
    shared_b_blocks = shared_b.reshape(span_count, block_len, shared_b.shape[1])
    scores = jnp.einsum(
        "ktn,ksn->kts", shared_c_blocks, shared_b_blocks, preferred_element_type=jnp.float32
    )
    weighted = decay_mat * scores[None]
    to_end = jnp.exp(totals[:, :, None] - cumlog).transpose(1, 2, 0)
    from_start = jnp.exp(cumlog).transpose(1, 2, 0)
    scaled_x = values_f * to_end[..., None]
    local_states = jnp.einsum("ksn,kshp->khnp", shared_bf, scaled_x, precision=highest)
    span_decay = jnp.exp(totals).T

    def forward_step(running, inputs):
        decay_k, local_k = inputs
        return (decay_k[:, None, None] * running + local_k, running)

    _, entries = lax.scan(forward_step, entry, (span_decay, local_states))
    ssm_out = jnp.einsum("hkts,kshp->kthp", weighted, values_f, precision=highest)
    ssm_out = ssm_out + from_start[..., None] * jnp.einsum(
        "ktn,khnp->kthp", shared_cf, entries, precision=highest
    )
    gate_sig = jax.nn.sigmoid(gates_f)
    grad_y = grad_f * gates_f * gate_sig
    grad_z = grad_f * ssm_out * gate_sig * (1.0 + gates_f * (1.0 - gate_sig))
    products = decay_mat * jnp.einsum("kthp,kshp->hkts", grad_y, values_f, precision=highest)
    scaled_dy = grad_y * from_start[..., None]
    grad_c = jnp.einsum("hkts,ksn->ktn", products, shared_bf, precision=highest)
    grad_c = grad_c + jnp.einsum("kthp,khnp->ktn", scaled_dy, entries, precision=highest)
    grad_b = jnp.einsum("hkst,ksn->ktn", products, shared_cf, precision=highest)
    grad_x = jnp.einsum("hkst,kshp->kthp", weighted, grad_y, precision=highest)
    block_terms = jnp.einsum("ksn,kshp->khnp", shared_cf, scaled_dy, precision=highest)

    def backward_step(running, inputs):
        decay_k, term_k = inputs
        return (term_k + decay_k[:, None, None] * running, running)

    block_sum, later_sums = lax.scan(
        backward_step, jnp.zeros_like(entry), (span_decay, block_terms), reverse=True
    )
    block_log = jnp.sum(totals, axis=1)
    suffix = block_log[None, :] - jnp.cumsum(totals, axis=1).T
    grad_z_out = grad_z.reshape(length, head_count * head_width).astype(jnp.bfloat16)
    return (
        grad_z_out,
        grad_x,
        grad_b,
        grad_c,
        later_sums,
        suffix,
        to_end,
        scaled_x,
        shared_bf,
        block_sum,
        block_log,
    )


def finish_block(partials, incoming):
    (
        grad_z_out,
        grad_x,
        grad_b,
        grad_c,
        later_sums,
        suffix,
        to_end,
        scaled_x,
        shared_bf,
        block_sum,
        block_log,
    ) = partials
    carried = later_sums + jnp.exp(suffix)[:, :, None, None] * incoming[None]
    grad_x = grad_x + to_end[..., None] * jnp.einsum(
        "ktn,khnp->kthp", shared_bf, carried, precision=highest
    )
    grad_b = grad_b + jnp.einsum("kthp,khnp->ktn", scaled_x, carried, precision=highest)
    length = grad_z_out.shape[0]
    grad_x_out = grad_x.reshape(length, grad_z_out.shape[1]).astype(jnp.bfloat16)
    grad_bc = jnp.concatenate([grad_b.reshape(length, -1), grad_c.reshape(length, -1)], axis=1)
    return (grad_z_out, grad_x_out, grad_bc)


def times_rows(left, weights):
    return lax.dot_general(
        left, weights, (((1,), (1,)), ((), ())), preferred_element_type=jnp.float32
    )


def row_term(events, projected, norm_scale):
    return (
        lax.dot_general(
            events, projected, (((0,), (0,)), ((), ())), preferred_element_type=jnp.float32
        )
        * norm_scale
    )


def summed_over(part, axis, split):
    gathered = lax.all_to_all(part, axis, split, split, tiled=True)
    shape = gathered.shape
    pieces = shape[:split] + (lax.axis_size(axis), shape[split] // lax.axis_size(axis)) + shape[split + 1 :]
    return jnp.sum(gathered.astype(jnp.float32).reshape(pieces), axis=split)


def per_device(
    events,
    ssm_input,
    gate_input,
    grad_out,
    shared_b,
    shared_c,
    log_decay,
    entry_state,
    w_gate,
    w_value,
    w_shared,
):
    partials = ssd_partials(
        ssm_input, gate_input, grad_out, shared_b, shared_c, log_decay, entry_state[0], SPAN
    )
    block_sum = partials[9]
    block_log = partials[10]
    _, incoming = suffix_scan((jnp.exp(block_log), block_sum), CTX)
    grad_z, grad_x, grad_bc_part = finish_block(partials, incoming)
    grad_bc = summed_over(grad_bc_part, HEAD, 1).astype(jnp.bfloat16)
    input_part = (
        times_rows(grad_z, w_gate) + times_rows(grad_x, w_value) + times_rows(grad_bc, w_shared)
    )
    grad_input = summed_over(input_part.astype(jnp.bfloat16), HEAD, 1).astype(jnp.bfloat16)
    norm_scale = 1.0 / math.sqrt(events.shape[0] * lax.axis_size(CTX))
    head_cols = grad_z.shape[1]
    projected = jnp.concatenate([grad_z, grad_x, grad_bc], axis=1)
    rows = row_term(events, projected, norm_scale)
    sizes = [lax.axis_size(name) for name in CTX]
    rows = rows.reshape(*sizes, rows.shape[0] // math.prod(sizes), rows.shape[1])
    for level in reversed(range(len(CTX))):
        rows = summed_over(rows, CTX[level], level)
    reduced = rows.reshape(rows.shape[-2], rows.shape[-1])
    grad_w_gate = reduced[:, :head_cols]
    grad_w_value = reduced[:, head_cols : 2 * head_cols]
    grad_w_shared = reduced[:, 2 * head_cols :]
    return (grad_input, grad_w_gate, grad_w_value, grad_w_shared)


CTX = ("z", "y_lo", "core")
HEAD = ("y_hi", "x")


def solution(mesh):
    ctx_size, head_size = mesh.devices.shape
    z_size = ctx_size // 4
    fine = jax.sharding.Mesh(
        mesh.devices.reshape(z_size, 2, 2, 2, head_size // 2),
        CTX + HEAD,
    )
    rows = P(CTX, None)
    both = P(CTX, HEAD)
    placed = (
        rows,
        both,
        both,
        both,
        rows,
        rows,
        P(HEAD, CTX),
        P(CTX, HEAD, None, None),
        P(None, HEAD),
        P(None, HEAD),
        P(None, HEAD),
    )
    return jax.shard_map(
        per_device,
        mesh=fine,
        in_specs=placed,
        out_specs=(both, both, both, both),
        check_vma=False,
    )
```

```python
import math

import jax
import jax.numpy as jnp
from jax import lax
from jax.sharding import PartitionSpec as P

SPAN = 256


highest = lax.Precision.HIGHEST


def suffix_scan(part, axis):
    count = lax.axis_size(axis)
    place = lax.axis_index(axis)

    def shifted(tree, step):
        pairs = [(source, source - step) for source in range(step, count)]
        return jax.tree.map(lambda a: lax.ppermute(a, axis, pairs), tree)

    def combine(near, far):
        return (near[0] * far[0], near[1] + near[0][:, None, None] * far[1])

    state = shifted(part, 1)
    valid = place + 1 < count
    state = (jnp.where(valid, state[0], 1.0), jnp.where(valid, state[1], 0.0))
    step = 1
    while step < count:
        far = shifted(state, step)
        joined = combine(state, far)
        inside = place + step < count
        state = (
            jnp.where(inside, joined[0], state[0]),
            jnp.where(inside, joined[1], state[1]),
        )
        step *= 2
    return state


def ssd_partials(ssm_input, gate_input, grad_out, shared_b, shared_c, log_decay, entry, block_len):
    head_count, length = log_decay.shape
    head_width = ssm_input.shape[1] // head_count
    span_count = length // block_len
    values_f = ssm_input.astype(jnp.float32).reshape(span_count, block_len, head_count, head_width)
    gates_f = gate_input.astype(jnp.float32).reshape(span_count, block_len, head_count, head_width)
    grad_f = grad_out.astype(jnp.float32).reshape(span_count, block_len, head_count, head_width)
    shared_bf = shared_b.astype(jnp.float32).reshape(span_count, block_len, shared_b.shape[1])
    shared_cf = shared_c.astype(jnp.float32).reshape(span_count, block_len, shared_c.shape[1])
    cumlog = jnp.cumsum(log_decay.reshape(head_count, span_count, block_len), axis=2)
    totals = cumlog[:, :, -1]
    causal = jnp.arange(block_len)[:, None] >= jnp.arange(block_len)[None, :]
    spread = cumlog[:, :, :, None] - cumlog[:, :, None, :]
    decay_mat = jnp.where(causal, jnp.exp(jnp.minimum(spread, 0.0)), 0.0)
    shared_c_blocks = shared_c.reshape(span_count, block_len, shared_c.shape[1])
    shared_b_blocks = shared_b.reshape(span_count, block_len, shared_b.shape[1])
    scores = jnp.einsum(
        "ktn,ksn->kts", shared_c_blocks, shared_b_blocks, preferred_element_type=jnp.float32
    )
    weighted = decay_mat * scores[None]
    to_end = jnp.exp(totals[:, :, None] - cumlog).transpose(1, 2, 0)
    from_start = jnp.exp(cumlog).transpose(1, 2, 0)
    scaled_x = values_f * to_end[..., None]
    local_states = jnp.einsum("ksn,kshp->khnp", shared_bf, scaled_x, precision=highest)
    span_decay = jnp.exp(totals).T

    def forward_step(running, inputs):
        decay_k, local_k = inputs
        return (decay_k[:, None, None] * running + local_k, running)

    _, entries = lax.scan(forward_step, entry, (span_decay, local_states))
    ssm_out = jnp.einsum("hkts,kshp->kthp", weighted, values_f, precision=highest)
    ssm_out = ssm_out + from_start[..., None] * jnp.einsum(
        "ktn,khnp->kthp", shared_cf, entries, precision=highest
    )
    gate_sig = jax.nn.sigmoid(gates_f)
    grad_y = grad_f * gates_f * gate_sig
    grad_z = grad_f * ssm_out * gate_sig * (1.0 + gates_f * (1.0 - gate_sig))
    products = decay_mat * jnp.einsum("kthp,kshp->hkts", grad_y, values_f, precision=highest)
    scaled_dy = grad_y * from_start[..., None]
    grad_c = jnp.einsum("hkts,ksn->ktn", products, shared_bf, precision=highest)
    grad_c = grad_c + jnp.einsum("kthp,khnp->ktn", scaled_dy, entries, precision=highest)
    grad_b = jnp.einsum("hkst,ksn->ktn", products, shared_cf, precision=highest)
    grad_x = jnp.einsum("hkst,kshp->kthp", weighted, grad_y, precision=highest)
    block_terms = jnp.einsum("ksn,kshp->khnp", shared_cf, scaled_dy, precision=highest)

    def backward_step(running, inputs):
        decay_k, term_k = inputs
        return (term_k + decay_k[:, None, None] * running, running)

    block_sum, later_sums = lax.scan(
        backward_step, jnp.zeros_like(entry), (span_decay, block_terms), reverse=True
    )
    block_log = jnp.sum(totals, axis=1)
    suffix = block_log[None, :] - jnp.cumsum(totals, axis=1).T
    grad_z_out = grad_z.reshape(length, head_count * head_width).astype(jnp.bfloat16)
    return (
        grad_z_out,
        grad_x,
        grad_b,
        grad_c,
        later_sums,
        suffix,
        to_end,
        scaled_x,
        shared_bf,
        block_sum,
        block_log,
    )


def finish_block(partials, incoming):
    (
        grad_z_out,
        grad_x,
        grad_b,
        grad_c,
        later_sums,
        suffix,
        to_end,
        scaled_x,
        shared_bf,
        block_sum,
        block_log,
    ) = partials
    carried = later_sums + jnp.exp(suffix)[:, :, None, None] * incoming[None]
    grad_x = grad_x + to_end[..., None] * jnp.einsum(
        "ktn,khnp->kthp", shared_bf, carried, precision=highest
    )
    grad_b = grad_b + jnp.einsum("kthp,khnp->ktn", scaled_x, carried, precision=highest)
    length = grad_z_out.shape[0]
    grad_x_out = grad_x.reshape(length, grad_z_out.shape[1]).astype(jnp.bfloat16)
    grad_bc = jnp.concatenate([grad_b.reshape(length, -1), grad_c.reshape(length, -1)], axis=1)
    return (grad_z_out, grad_x_out, grad_bc)


def times_rows(left, weights):
    return lax.dot_general(
        left, weights, (((1,), (1,)), ((), ())), preferred_element_type=jnp.float32
    )


def row_term(events, projected, norm_scale):
    return (
        lax.dot_general(
            events, projected, (((0,), (0,)), ((), ())), preferred_element_type=jnp.float32
        )
        * norm_scale
    )


def summed_over(part, axis, split):
    gathered = lax.all_to_all(part, axis, split, split, tiled=True)
    shape = gathered.shape
    pieces = shape[:split] + (lax.axis_size(axis), shape[split] // lax.axis_size(axis)) + shape[split + 1 :]
    return jnp.sum(gathered.astype(jnp.float32).reshape(pieces), axis=split)


def per_device(
    events,
    ssm_input,
    gate_input,
    grad_out,
    shared_b,
    shared_c,
    log_decay,
    entry_state,
    w_gate,
    w_value,
    w_shared,
):
    partials = ssd_partials(
        ssm_input, gate_input, grad_out, shared_b, shared_c, log_decay, entry_state[0], SPAN
    )
    block_sum = partials[9]
    block_log = partials[10]
    _, incoming = suffix_scan((jnp.exp(block_log), block_sum), CTX)
    grad_z, grad_x, grad_bc_part = finish_block(partials, incoming)
    grad_bc = summed_over(grad_bc_part, HEAD, 1).astype(jnp.bfloat16)
    input_part = (
        times_rows(grad_z, w_gate) + times_rows(grad_x, w_value) + times_rows(grad_bc, w_shared)
    )
    grad_input = summed_over(input_part.astype(jnp.bfloat16), HEAD, 1).astype(jnp.bfloat16)
    norm_scale = 1.0 / math.sqrt(events.shape[0] * lax.axis_size(CTX))
    head_cols = grad_z.shape[1]
    projected = jnp.concatenate([grad_z, grad_x, grad_bc], axis=1)
    rows = row_term(events, projected, norm_scale)
    sizes = [lax.axis_size(name) for name in CTX]
    rows = rows.reshape(*sizes, rows.shape[0] // math.prod(sizes), rows.shape[1])
    for level in reversed(range(len(CTX))):
        rows = summed_over(rows.astype(jnp.bfloat16), CTX[level], level)
    reduced = rows.reshape(rows.shape[-2], rows.shape[-1])
    grad_w_gate = reduced[:, :head_cols]
    grad_w_value = reduced[:, head_cols : 2 * head_cols]
    grad_w_shared = reduced[:, 2 * head_cols :]
    return (grad_input, grad_w_gate, grad_w_value, grad_w_shared)


CTX = ("z", "y_lo", "core")
HEAD = ("y_hi", "x")


def solution(mesh):
    ctx_size, head_size = mesh.devices.shape
    z_size = ctx_size // 4
    fine = jax.sharding.Mesh(
        mesh.devices.reshape(z_size, 2, 2, 2, head_size // 2),
        CTX + HEAD,
    )
    rows = P(CTX, None)
    both = P(CTX, HEAD)
    placed = (
        rows,
        both,
        both,
        both,
        rows,
        rows,
        P(HEAD, CTX),
        P(CTX, HEAD, None, None),
        P(None, HEAD),
        P(None, HEAD),
        P(None, HEAD),
    )
    return jax.shard_map(
        per_device,
        mesh=fine,
        in_specs=placed,
        out_specs=(both, both, both, both),
        check_vma=False,
    )
```

```python
import math

import jax
import jax.numpy as jnp
from jax import lax
from jax.sharding import PartitionSpec as P

SPAN = 256


highest = lax.Precision.HIGHEST


def join(near, far):
    return (near[0] * far[0], near[1] + near[0][..., None, None] * far[1])


def pick(flag, first, second):
    return jax.tree.map(lambda a, b: jnp.where(flag, a, b), first, second)


def swap(tree, axis):
    return jax.tree.map(lambda a: lax.ppermute(a, axis, [(0, 1), (1, 0)]), tree)


def shift(tree, axis, step):
    pairs = [(source, source - step) for source in range(step, lax.axis_size(axis))]
    return jax.tree.map(lambda a: lax.ppermute(a, axis, pairs), tree)


def suffix_scan(part):
    z_axis, pair_axis, core_axis = CTX
    core = lax.axis_index(core_axis)
    pair = lax.axis_index(pair_axis)
    plane = pair * 2 + core
    identity = jax.tree.map(lambda a: jnp.zeros_like(a) + jnp.asarray(1.0 if a.ndim == 1 else 0.0, a.dtype), part)
    other = swap(part, core_axis)
    pair_total = pick(core == 0, join(part, other), join(other, part))
    other_pair = swap(pair_total, pair_axis)
    total = pick(pair == 0, join(pair_total, other_pair), join(other_pair, pair_total))
    within = join(pick(core == 0, other, identity), pick(pair == 0, other_pair, identity))
    head = (
        lax.dynamic_index_in_dim(total[0], plane, 0, False),
        lax.dynamic_index_in_dim(total[1], plane, 0, False),
    )
    one = (jnp.ones_like(head[0]), jnp.zeros_like(head[1]))
    z = lax.axis_index(z_axis)
    count = lax.axis_size(z_axis)
    near = pick(z + 1 < count, shift(head, z_axis, 1), one)
    far = pick(z + 2 < count, shift(head, z_axis, 2), one)
    later = join(near, far)
    step = 2
    while step < count:
        later = pick(z + step < count, join(later, shift(later, z_axis, step)), later)
        step *= 2
    mine = later[1]
    theirs = swap(mine, core_axis)
    two = jnp.where(core == 0, jnp.stack([mine, theirs]), jnp.stack([theirs, mine]))
    two_other = swap(two, pair_axis)
    four = jnp.where(pair == 0, jnp.concatenate([two, two_other]), jnp.concatenate([two_other, two]))
    return within[1] + within[0][:, None, None] * four


def ssd_partials(ssm_input, gate_input, grad_out, shared_b, shared_c, log_decay, entry, block_len):
    head_count, length = log_decay.shape
    head_width = ssm_input.shape[1] // head_count
    span_count = length // block_len
    values_f = ssm_input.astype(jnp.float32).reshape(span_count, block_len, head_count, head_width)
    gates_f = gate_input.astype(jnp.float32).reshape(span_count, block_len, head_count, head_width)
    grad_f = grad_out.astype(jnp.float32).reshape(span_count, block_len, head_count, head_width)
    shared_bf = shared_b.astype(jnp.float32).reshape(span_count, block_len, shared_b.shape[1])
    shared_cf = shared_c.astype(jnp.float32).reshape(span_count, block_len, shared_c.shape[1])
    cumlog = jnp.cumsum(log_decay.reshape(head_count, span_count, block_len), axis=2)
    totals = cumlog[:, :, -1]
    causal = jnp.arange(block_len)[:, None] >= jnp.arange(block_len)[None, :]
    spread = cumlog[:, :, :, None] - cumlog[:, :, None, :]
    decay_mat = jnp.where(causal, jnp.exp(jnp.minimum(spread, 0.0)), 0.0)
    shared_c_blocks = shared_c.reshape(span_count, block_len, shared_c.shape[1])
    shared_b_blocks = shared_b.reshape(span_count, block_len, shared_b.shape[1])
    scores = jnp.einsum(
        "ktn,ksn->kts", shared_c_blocks, shared_b_blocks, preferred_element_type=jnp.float32
    )
    weighted = decay_mat * scores[None]
    to_end = jnp.exp(totals[:, :, None] - cumlog).transpose(1, 2, 0)
    from_start = jnp.exp(cumlog).transpose(1, 2, 0)
    scaled_x = values_f * to_end[..., None]
    local_states = jnp.einsum("ksn,kshp->khnp", shared_bf, scaled_x, precision=highest)
    span_decay = jnp.exp(totals).T

    def forward_step(running, inputs):
        decay_k, local_k = inputs
        return (decay_k[:, None, None] * running + local_k, running)

    _, entries = lax.scan(forward_step, entry, (span_decay, local_states))
    ssm_out = jnp.einsum("hkts,kshp->kthp", weighted, values_f, precision=highest)
    ssm_out = ssm_out + from_start[..., None] * jnp.einsum(
        "ktn,khnp->kthp", shared_cf, entries, precision=highest
    )
    gate_sig = jax.nn.sigmoid(gates_f)
    grad_y = grad_f * gates_f * gate_sig
    grad_z = grad_f * ssm_out * gate_sig * (1.0 + gates_f * (1.0 - gate_sig))
    products = decay_mat * jnp.einsum("kthp,kshp->hkts", grad_y, values_f, precision=highest)
    scaled_dy = grad_y * from_start[..., None]
    grad_c = jnp.einsum("hkts,ksn->ktn", products, shared_bf, precision=highest)
    grad_c = grad_c + jnp.einsum("kthp,khnp->ktn", scaled_dy, entries, precision=highest)
    grad_b = jnp.einsum("hkst,ksn->ktn", products, shared_cf, precision=highest)
    grad_x = jnp.einsum("hkst,kshp->kthp", weighted, grad_y, precision=highest)
    block_terms = jnp.einsum("ksn,kshp->khnp", shared_cf, scaled_dy, precision=highest)

    def backward_step(running, inputs):
        decay_k, term_k = inputs
        return (term_k + decay_k[:, None, None] * running, running)

    block_sum, later_sums = lax.scan(
        backward_step, jnp.zeros_like(entry), (span_decay, block_terms), reverse=True
    )
    block_log = jnp.sum(totals, axis=1)
    suffix = block_log[None, :] - jnp.cumsum(totals, axis=1).T
    grad_z_out = grad_z.reshape(length, head_count * head_width).astype(jnp.bfloat16)
    return (
        grad_z_out,
        grad_x,
        grad_b,
        grad_c,
        later_sums,
        suffix,
        to_end,
        scaled_x,
        shared_bf,
        block_sum,
        block_log,
    )


def finish_block(partials, incoming):
    (
        grad_z_out,
        grad_x,
        grad_b,
        grad_c,
        later_sums,
        suffix,
        to_end,
        scaled_x,
        shared_bf,
        block_sum,
        block_log,
    ) = partials
    carried = later_sums + jnp.exp(suffix)[:, :, None, None] * incoming[None]
    grad_x = grad_x + to_end[..., None] * jnp.einsum(
        "ktn,khnp->kthp", shared_bf, carried, precision=highest
    )
    grad_b = grad_b + jnp.einsum("kthp,khnp->ktn", scaled_x, carried, precision=highest)
    length = grad_z_out.shape[0]
    grad_x_out = grad_x.reshape(length, grad_z_out.shape[1]).astype(jnp.bfloat16)
    grad_bc = jnp.concatenate([grad_b.reshape(length, -1), grad_c.reshape(length, -1)], axis=1)
    return (grad_z_out, grad_x_out, grad_bc)


def times_rows(left, weights):
    return lax.dot_general(
        left, weights, (((1,), (1,)), ((), ())), preferred_element_type=jnp.float32
    )


def row_term(events, projected, norm_scale):
    return (
        lax.dot_general(
            events, projected, (((0,), (0,)), ((), ())), preferred_element_type=jnp.float32
        )
        * norm_scale
    )


def summed_over(part, axis, split):
    gathered = lax.all_to_all(part, axis, split, split, tiled=True)
    shape = gathered.shape
    pieces = shape[:split] + (lax.axis_size(axis), shape[split] // lax.axis_size(axis)) + shape[split + 1 :]
    return jnp.sum(gathered.astype(jnp.float32).reshape(pieces), axis=split)


def per_device(
    events,
    ssm_input,
    gate_input,
    grad_out,
    shared_b,
    shared_c,
    log_decay,
    entry_state,
    w_gate,
    w_value,
    w_shared,
):
    partials = ssd_partials(
        ssm_input, gate_input, grad_out, shared_b, shared_c, log_decay, entry_state[0], SPAN
    )
    block_sum = partials[9]
    block_log = partials[10]
    incoming = suffix_scan((jnp.exp(block_log), block_sum))
    grad_z, grad_x, grad_bc_part = finish_block(partials, incoming)
    grad_bc = summed_over(grad_bc_part, HEAD, 1).astype(jnp.bfloat16)
    input_part = (
        times_rows(grad_z, w_gate) + times_rows(grad_x, w_value) + times_rows(grad_bc, w_shared)
    )
    grad_input = summed_over(input_part.astype(jnp.bfloat16), HEAD, 1).astype(jnp.bfloat16)
    norm_scale = 1.0 / math.sqrt(events.shape[0] * lax.axis_size(CTX))
    head_cols = grad_z.shape[1]
    projected = jnp.concatenate([grad_z, grad_x, grad_bc], axis=1)
    rows = row_term(events, projected, norm_scale)
    sizes = [lax.axis_size(name) for name in CTX]
    rows = rows.reshape(*sizes, rows.shape[0] // math.prod(sizes), rows.shape[1])
    for level in reversed(range(len(CTX))):
        rows = summed_over(rows.astype(jnp.bfloat16), CTX[level], level)
    reduced = rows.reshape(rows.shape[-2], rows.shape[-1])
    grad_w_gate = reduced[:, :head_cols]
    grad_w_value = reduced[:, head_cols : 2 * head_cols]
    grad_w_shared = reduced[:, 2 * head_cols :]
    return (grad_input, grad_w_gate, grad_w_value, grad_w_shared)


CTX = ("z", "y_lo", "core")
HEAD = ("y_hi", "x")


def solution(mesh):
    ctx_size, head_size = mesh.devices.shape
    z_size = ctx_size // 4
    fine = jax.sharding.Mesh(
        mesh.devices.reshape(z_size, 2, 2, 2, head_size // 2),
        CTX + HEAD,
    )
    rows = P(CTX, None)
    both = P(CTX, HEAD)
    placed = (
        rows,
        both,
        both,
        both,
        rows,
        rows,
        P(HEAD, CTX),
        P(CTX, HEAD, None, None),
        P(None, HEAD),
        P(None, HEAD),
        P(None, HEAD),
    )
    return jax.shard_map(
        per_device,
        mesh=fine,
        in_specs=placed,
        out_specs=(both, both, both, both),
        check_vma=False,
    )
```

```python
import math

import jax
import jax.numpy as jnp
from jax import lax
from jax.sharding import PartitionSpec as P

SPAN = 256


highest = lax.Precision.HIGHEST


def join(near, far):
    return (near[0] * far[0], near[1] + near[0][..., None, None] * far[1])


def pick(flag, first, second):
    return jax.tree.map(lambda a, b: jnp.where(flag, a, b), first, second)


def packed(pair):
    rows = jnp.broadcast_to(pair[0][..., None, None], pair[0].shape + (8, pair[1].shape[-1]))
    return jnp.concatenate([pair[1], rows], axis=-2)


def unpacked(block):
    return (block[..., -8, 0], block[..., :-8, :])


def rolled(block, axis, step):
    count = lax.axis_size(axis)
    return lax.ppermute(block, axis, [(source, (source - step) % count) for source in range(count)])


def fold(parts):
    total = parts[0]
    for part in parts[1:]:
        total = join(total, part)
    return total


def suffix_scan(part):
    z_axis = CTX[0]
    plane_axis = CTX[1:]
    plane = lax.axis_index(plane_axis)
    width = lax.axis_size(plane_axis)
    own = packed(part)
    got = [own] + [rolled(own, plane_axis, step) for step in range(1, width)]
    pairs = [unpacked(block) for block in got]
    identity = (jnp.ones_like(part[0]), jnp.zeros_like(part[1]))
    within = fold([pick(plane + step < width, pairs[step], identity) for step in range(1, width)])
    stacked = jnp.stack([lax.dynamic_index_in_dim(block, plane, 0, False) for block in got])
    by_place = [
        unpacked(lax.dynamic_index_in_dim(stacked, (place - plane) % width, 0, False))
        for place in range(width)
    ]
    total = fold(by_place)
    one = (jnp.ones_like(total[0]), jnp.zeros_like(total[1]))
    z = lax.axis_index(z_axis)
    count = lax.axis_size(z_axis)
    radix = 4
    span = 1
    later = None
    while span < count:
        source = packed(total) if later is None else packed(later)
        base = one if later is None else later
        parts = [base] if later is not None else []
        for k in range(1, radix + (1 if later is None else 0)):
            step = k * span
            if step >= count:
                break
            pairs_k = [(s, s - step) for s in range(step, count)]
            parts.append(pick(z + step < count, unpacked(lax.ppermute(source, z_axis, pairs_k)), one))
        later = fold(parts)
        span *= radix
    mine = later[1]
    gathered = [mine] + [rolled(mine, plane_axis, step) for step in range(1, width)]
    block = jnp.stack(gathered)
    four = jnp.stack(
        [lax.dynamic_index_in_dim(block, (place - plane) % width, 0, False) for place in range(width)]
    )
    return within[1] + within[0][:, None, None] * four


def ssd_partials(ssm_input, gate_input, grad_out, shared_b, shared_c, log_decay, entry, block_len):
    head_count, length = log_decay.shape
    head_width = ssm_input.shape[1] // head_count
    span_count = length // block_len
    values_f = ssm_input.astype(jnp.float32).reshape(span_count, block_len, head_count, head_width)
    gates_f = gate_input.astype(jnp.float32).reshape(span_count, block_len, head_count, head_width)
    grad_f = grad_out.astype(jnp.float32).reshape(span_count, block_len, head_count, head_width)
    shared_bf = shared_b.astype(jnp.float32).reshape(span_count, block_len, shared_b.shape[1])
    shared_cf = shared_c.astype(jnp.float32).reshape(span_count, block_len, shared_c.shape[1])
    cumlog = jnp.cumsum(log_decay.reshape(head_count, span_count, block_len), axis=2)
    totals = cumlog[:, :, -1]
    causal = jnp.arange(block_len)[:, None] >= jnp.arange(block_len)[None, :]
    spread = cumlog[:, :, :, None] - cumlog[:, :, None, :]
    decay_mat = jnp.where(causal, jnp.exp(jnp.minimum(spread, 0.0)), 0.0)
    shared_c_blocks = shared_c.reshape(span_count, block_len, shared_c.shape[1])
    shared_b_blocks = shared_b.reshape(span_count, block_len, shared_b.shape[1])
    scores = jnp.einsum(
        "ktn,ksn->kts", shared_c_blocks, shared_b_blocks, preferred_element_type=jnp.float32
    )
    weighted = decay_mat * scores[None]
    to_end = jnp.exp(totals[:, :, None] - cumlog).transpose(1, 2, 0)
    from_start = jnp.exp(cumlog).transpose(1, 2, 0)
    scaled_x = values_f * to_end[..., None]
    local_states = jnp.einsum("ksn,kshp->khnp", shared_bf, scaled_x, precision=highest)
    span_decay = jnp.exp(totals).T

    def forward_step(running, inputs):
        decay_k, local_k = inputs
        return (decay_k[:, None, None] * running + local_k, running)

    _, entries = lax.scan(forward_step, entry, (span_decay, local_states))
    ssm_out = jnp.einsum("hkts,kshp->kthp", weighted, values_f, precision=highest)
    ssm_out = ssm_out + from_start[..., None] * jnp.einsum(
        "ktn,khnp->kthp", shared_cf, entries, precision=highest
    )
    gate_sig = jax.nn.sigmoid(gates_f)
    grad_y = grad_f * gates_f * gate_sig
    grad_z = grad_f * ssm_out * gate_sig * (1.0 + gates_f * (1.0 - gate_sig))
    products = decay_mat * jnp.einsum("kthp,kshp->hkts", grad_y, values_f, precision=highest)
    scaled_dy = grad_y * from_start[..., None]
    grad_c = jnp.einsum("hkts,ksn->ktn", products, shared_bf, precision=highest)
    grad_c = grad_c + jnp.einsum("kthp,khnp->ktn", scaled_dy, entries, precision=highest)
    grad_b = jnp.einsum("hkst,ksn->ktn", products, shared_cf, precision=highest)
    grad_x = jnp.einsum("hkst,kshp->kthp", weighted, grad_y, precision=highest)
    block_terms = jnp.einsum("ksn,kshp->khnp", shared_cf, scaled_dy, precision=highest)

    def backward_step(running, inputs):
        decay_k, term_k = inputs
        return (term_k + decay_k[:, None, None] * running, running)

    block_sum, later_sums = lax.scan(
        backward_step, jnp.zeros_like(entry), (span_decay, block_terms), reverse=True
    )
    block_log = jnp.sum(totals, axis=1)
    suffix = block_log[None, :] - jnp.cumsum(totals, axis=1).T
    grad_z_out = grad_z.reshape(length, head_count * head_width).astype(jnp.bfloat16)
    return (
        grad_z_out,
        grad_x,
        grad_b,
        grad_c,
        later_sums,
        suffix,
        to_end,
        scaled_x,
        shared_bf,
        block_sum,
        block_log,
    )


def finish_block(partials, incoming):
    (
        grad_z_out,
        grad_x,
        grad_b,
        grad_c,
        later_sums,
        suffix,
        to_end,
        scaled_x,
        shared_bf,
        block_sum,
        block_log,
    ) = partials
    carried = later_sums + jnp.exp(suffix)[:, :, None, None] * incoming[None]
    grad_x = grad_x + to_end[..., None] * jnp.einsum(
        "ktn,khnp->kthp", shared_bf, carried, precision=highest
    )
    grad_b = grad_b + jnp.einsum("kthp,khnp->ktn", scaled_x, carried, precision=highest)
    length = grad_z_out.shape[0]
    grad_x_out = grad_x.reshape(length, grad_z_out.shape[1]).astype(jnp.bfloat16)
    grad_bc = jnp.concatenate([grad_b.reshape(length, -1), grad_c.reshape(length, -1)], axis=1)
    return (grad_z_out, grad_x_out, grad_bc)


def times_rows(left, weights):
    return lax.dot_general(
        left, weights, (((1,), (1,)), ((), ())), preferred_element_type=jnp.float32
    )


def row_term(events, projected, norm_scale):
    return (
        lax.dot_general(
            events, projected, (((0,), (0,)), ((), ())), preferred_element_type=jnp.float32
        )
        * norm_scale
    )


def summed_over(part, axis, split):
    gathered = lax.all_to_all(part, axis, split, split, tiled=True)
    shape = gathered.shape
    pieces = shape[:split] + (lax.axis_size(axis), shape[split] // lax.axis_size(axis)) + shape[split + 1 :]
    return jnp.sum(gathered.astype(jnp.float32).reshape(pieces), axis=split)


def per_device(
    events,
    ssm_input,
    gate_input,
    grad_out,
    shared_b,
    shared_c,
    log_decay,
    entry_state,
    w_gate,
    w_value,
    w_shared,
):
    partials = ssd_partials(
        ssm_input, gate_input, grad_out, shared_b, shared_c, log_decay, entry_state[0], SPAN
    )
    block_sum = partials[9]
    block_log = partials[10]
    incoming = suffix_scan((jnp.exp(block_log), block_sum))
    grad_z, grad_x, grad_bc_part = finish_block(partials, incoming)
    grad_bc = summed_over(grad_bc_part, HEAD, 1).astype(jnp.bfloat16)
    input_part = (
        times_rows(grad_z, w_gate) + times_rows(grad_x, w_value) + times_rows(grad_bc, w_shared)
    )
    grad_input = summed_over(input_part.astype(jnp.bfloat16), HEAD, 1).astype(jnp.bfloat16)
    norm_scale = 1.0 / math.sqrt(events.shape[0] * lax.axis_size(CTX))
    head_cols = grad_z.shape[1]
    projected = jnp.concatenate([grad_z, grad_x, grad_bc], axis=1)
    rows = row_term(events, projected, norm_scale)
    sizes = [lax.axis_size(name) for name in CTX]
    rows = rows.reshape(*sizes, rows.shape[0] // math.prod(sizes), rows.shape[1])
    for level in reversed(range(len(CTX))):
        rows = summed_over(rows.astype(jnp.bfloat16), CTX[level], level)
    reduced = rows.reshape(rows.shape[-2], rows.shape[-1])
    grad_w_gate = reduced[:, :head_cols]
    grad_w_value = reduced[:, head_cols : 2 * head_cols]
    grad_w_shared = reduced[:, 2 * head_cols :]
    return (grad_input, grad_w_gate, grad_w_value, grad_w_shared)


CTX = ("z", "y_lo", "core")
HEAD = ("y_hi", "x")


def solution(mesh):
    ctx_size, head_size = mesh.devices.shape
    z_size = ctx_size // 4
    fine = jax.sharding.Mesh(
        mesh.devices.reshape(z_size, 2, 2, 2, head_size // 2),
        CTX + HEAD,
    )
    rows = P(CTX, None)
    both = P(CTX, HEAD)
    placed = (
        rows,
        both,
        both,
        both,
        rows,
        rows,
        P(HEAD, CTX),
        P(CTX, HEAD, None, None),
        P(None, HEAD),
        P(None, HEAD),
        P(None, HEAD),
    )
    return jax.shard_map(
        per_device,
        mesh=fine,
        in_specs=placed,
        out_specs=(both, both, both, both),
        check_vma=False,
    )
```

```python
import math

import jax
import jax.numpy as jnp
from jax import lax
from jax.sharding import PartitionSpec as P

SPAN = 256


highest = lax.Precision.HIGHEST


def join(near, far):
    return (near[0] * far[0], near[1] + near[0][..., None, None] * far[1])


def pick(flag, first, second):
    return jax.tree.map(lambda a, b: jnp.where(flag, a, b), first, second)


def swap(tree, axis):
    return jax.tree.map(lambda a: lax.ppermute(a, axis, [(0, 1), (1, 0)]), tree)


def shift(tree, axis, step):
    pairs = [(source, source - step) for source in range(step, lax.axis_size(axis))]
    return jax.tree.map(lambda a: lax.ppermute(a, axis, pairs), tree)


def suffix_scan(part):
    z_axis, pair_axis, core_axis = CTX
    core = lax.axis_index(core_axis)
    pair = lax.axis_index(pair_axis)
    plane = pair * 2 + core
    identity = jax.tree.map(lambda a: jnp.zeros_like(a) + jnp.asarray(1.0 if a.ndim == 1 else 0.0, a.dtype), part)
    other = swap(part, core_axis)
    pair_total = pick(core == 0, join(part, other), join(other, part))
    other_pair = swap(pair_total, pair_axis)
    total = pick(pair == 0, join(pair_total, other_pair), join(other_pair, pair_total))
    within = join(pick(core == 0, other, identity), pick(pair == 0, other_pair, identity))
    head = (
        lax.dynamic_index_in_dim(total[0], plane, 0, False),
        lax.dynamic_index_in_dim(total[1], plane, 0, False),
    )
    one = (jnp.ones_like(head[0]), jnp.zeros_like(head[1]))
    z = lax.axis_index(z_axis)
    count = lax.axis_size(z_axis)
    near = pick(z + 1 < count, shift(head, z_axis, 1), one)
    far = pick(z + 2 < count, shift(head, z_axis, 2), one)
    later = join(near, far)
    step = 2
    while step < count:
        later = pick(z + step < count, join(later, shift(later, z_axis, step)), later)
        step *= 2
    mine = later[1]
    theirs = swap(mine, core_axis)
    two = jnp.where(core == 0, jnp.stack([mine, theirs]), jnp.stack([theirs, mine]))
    two_other = swap(two, pair_axis)
    four = jnp.where(pair == 0, jnp.concatenate([two, two_other]), jnp.concatenate([two_other, two]))
    return within[1] + within[0][:, None, None] * four


def ssd_partials(ssm_input, gate_input, grad_out, shared_b, shared_c, log_decay, entry, block_len):
    head_count, length = log_decay.shape
    head_width = ssm_input.shape[1] // head_count
    span_count = length // block_len
    values_f = ssm_input.astype(jnp.float32).reshape(span_count, block_len, head_count, head_width)
    gates_f = gate_input.astype(jnp.float32).reshape(span_count, block_len, head_count, head_width)
    grad_f = grad_out.astype(jnp.float32).reshape(span_count, block_len, head_count, head_width)
    shared_bf = shared_b.astype(jnp.float32).reshape(span_count, block_len, shared_b.shape[1])
    shared_cf = shared_c.astype(jnp.float32).reshape(span_count, block_len, shared_c.shape[1])
    cumlog = jnp.cumsum(log_decay.reshape(head_count, span_count, block_len), axis=2)
    totals = cumlog[:, :, -1]
    causal = jnp.arange(block_len)[:, None] >= jnp.arange(block_len)[None, :]
    spread = cumlog[:, :, :, None] - cumlog[:, :, None, :]
    decay_mat = jnp.where(causal, jnp.exp(jnp.minimum(spread, 0.0)), 0.0)
    shared_c_blocks = shared_c.reshape(span_count, block_len, shared_c.shape[1])
    shared_b_blocks = shared_b.reshape(span_count, block_len, shared_b.shape[1])
    scores = jnp.einsum(
        "ktn,ksn->kts", shared_c_blocks, shared_b_blocks, preferred_element_type=jnp.float32
    )
    weighted = decay_mat * scores[None]
    to_end = jnp.exp(totals[:, :, None] - cumlog).transpose(1, 2, 0)
    from_start = jnp.exp(cumlog).transpose(1, 2, 0)
    scaled_x = values_f * to_end[..., None]
    local_states = jnp.einsum("ksn,kshp->khnp", shared_bf, scaled_x, precision=highest)
    span_decay = jnp.exp(totals).T

    def forward_step(running, inputs):
        decay_k, local_k = inputs
        return (decay_k[:, None, None] * running + local_k, running)

    _, entries = lax.scan(forward_step, entry, (span_decay, local_states))
    ssm_out = jnp.einsum("hkts,kshp->kthp", weighted, values_f, precision=highest)
    ssm_out = ssm_out + from_start[..., None] * jnp.einsum(
        "ktn,khnp->kthp", shared_cf, entries, precision=highest
    )
    gate_sig = jax.nn.sigmoid(gates_f)
    grad_y = grad_f * gates_f * gate_sig
    grad_z = grad_f * ssm_out * gate_sig * (1.0 + gates_f * (1.0 - gate_sig))
    products = decay_mat * jnp.einsum("kthp,kshp->hkts", grad_y, values_f, precision=highest)
    scaled_dy = grad_y * from_start[..., None]
    grad_c = jnp.einsum("hkts,ksn->ktn", products, shared_bf, precision=highest)
    grad_c = grad_c + jnp.einsum("kthp,khnp->ktn", scaled_dy, entries, precision=highest)
    grad_b = jnp.einsum("hkst,ksn->ktn", products, shared_cf, precision=highest)
    grad_x = jnp.einsum("hkst,kshp->kthp", weighted, grad_y, precision=highest)
    block_terms = jnp.einsum("ksn,kshp->khnp", shared_cf, scaled_dy, precision=highest)

    def backward_step(running, inputs):
        decay_k, term_k = inputs
        return (term_k + decay_k[:, None, None] * running, running)

    block_sum, later_sums = lax.scan(
        backward_step, jnp.zeros_like(entry), (span_decay, block_terms), reverse=True
    )
    block_log = jnp.sum(totals, axis=1)
    suffix = block_log[None, :] - jnp.cumsum(totals, axis=1).T
    grad_z_out = grad_z.reshape(length, head_count * head_width).astype(jnp.bfloat16)
    return (
        grad_z_out,
        grad_x,
        grad_b,
        grad_c,
        later_sums,
        suffix,
        to_end,
        scaled_x,
        shared_bf,
        block_sum,
        block_log,
    )


def finish_block(partials, incoming):
    (
        grad_z_out,
        grad_x,
        grad_b,
        grad_c,
        later_sums,
        suffix,
        to_end,
        scaled_x,
        shared_bf,
        block_sum,
        block_log,
    ) = partials
    carried = later_sums + jnp.exp(suffix)[:, :, None, None] * incoming[None]
    grad_x = grad_x + to_end[..., None] * jnp.einsum(
        "ktn,khnp->kthp", shared_bf, carried, precision=highest
    )
    grad_b = grad_b + jnp.einsum("kthp,khnp->ktn", scaled_x, carried, precision=highest)
    length = grad_z_out.shape[0]
    grad_x_out = grad_x.reshape(length, grad_z_out.shape[1]).astype(jnp.bfloat16)
    grad_bc = jnp.concatenate([grad_b.reshape(length, -1), grad_c.reshape(length, -1)], axis=1)
    return (grad_z_out, grad_x_out, grad_bc)


def times_rows(left, weights):
    return lax.dot_general(
        left, weights, (((1,), (1,)), ((), ())), preferred_element_type=jnp.float32
    )


def row_term(events, projected, norm_scale):
    return (
        lax.dot_general(
            events, projected, (((0,), (0,)), ((), ())), preferred_element_type=jnp.float32
        )
        * norm_scale
    )


def summed_over(part, axis, split):
    gathered = lax.all_to_all(part, axis, split, split, tiled=True)
    shape = gathered.shape
    pieces = shape[:split] + (lax.axis_size(axis), shape[split] // lax.axis_size(axis)) + shape[split + 1 :]
    return jnp.sum(gathered.astype(jnp.float32).reshape(pieces), axis=split)


def spread_sum(part, axis):
    count = lax.axis_size(axis)
    place = lax.axis_index(axis)
    chunks = part.reshape(part.shape[0], count, part.shape[1] // count).transpose(1, 0, 2)
    total = lax.dynamic_index_in_dim(chunks, place, 0, False).astype(jnp.float32)
    for step in range(1, count):
        piece = lax.dynamic_index_in_dim(chunks, (place - step) % count, 0, False)
        pairs = [(source, (source - step) % count) for source in range(count)]
        total = total + lax.ppermute(piece, axis, pairs).astype(jnp.float32)
    return total


def per_device(
    events,
    ssm_input,
    gate_input,
    grad_out,
    shared_b,
    shared_c,
    log_decay,
    entry_state,
    w_gate,
    w_value,
    w_shared,
):
    partials = ssd_partials(
        ssm_input, gate_input, grad_out, shared_b, shared_c, log_decay, entry_state[0], SPAN
    )
    block_sum = partials[9]
    block_log = partials[10]
    incoming = suffix_scan((jnp.exp(block_log), block_sum))
    grad_z, grad_x, grad_bc_part = finish_block(partials, incoming)
    grad_bc = summed_over(grad_bc_part, HEAD, 1).astype(jnp.bfloat16)
    input_part = (
        times_rows(grad_z, w_gate) + times_rows(grad_x, w_value) + times_rows(grad_bc, w_shared)
    )
    grad_input = spread_sum(input_part.astype(jnp.bfloat16), HEAD).astype(jnp.bfloat16)
    norm_scale = 1.0 / math.sqrt(events.shape[0] * lax.axis_size(CTX))
    head_cols = grad_z.shape[1]
    projected = jnp.concatenate([grad_z, grad_x, grad_bc], axis=1)
    rows = row_term(events, projected, norm_scale)
    sizes = [lax.axis_size(name) for name in CTX]
    rows = rows.reshape(*sizes, rows.shape[0] // math.prod(sizes), rows.shape[1])
    for level in reversed(range(len(CTX))):
        rows = summed_over(rows.astype(jnp.bfloat16), CTX[level], level)
    reduced = rows.reshape(rows.shape[-2], rows.shape[-1])
    grad_w_gate = reduced[:, :head_cols]
    grad_w_value = reduced[:, head_cols : 2 * head_cols]
    grad_w_shared = reduced[:, 2 * head_cols :]
    return (grad_input, grad_w_gate, grad_w_value, grad_w_shared)


CTX = ("z", "y_lo", "core")
HEAD = ("y_hi", "x")


def solution(mesh):
    ctx_size, head_size = mesh.devices.shape
    z_size = ctx_size // 4
    fine = jax.sharding.Mesh(
        mesh.devices.reshape(z_size, 2, 2, 2, head_size // 2),
        CTX + HEAD,
    )
    rows = P(CTX, None)
    both = P(CTX, HEAD)
    placed = (
        rows,
        both,
        both,
        both,
        rows,
        rows,
        P(HEAD, CTX),
        P(CTX, HEAD, None, None),
        P(None, HEAD),
        P(None, HEAD),
        P(None, HEAD),
    )
    return jax.shard_map(
        per_device,
        mesh=fine,
        in_specs=placed,
        out_specs=(both, both, both, both),
        check_vma=False,
    )
```

```python
import math

import jax
import jax.numpy as jnp
from jax import lax
from jax.sharding import PartitionSpec as P

SPAN = 256


highest = lax.Precision.HIGHEST


def join(near, far):
    return (near[0] * far[0], near[1] + near[0][..., None, None] * far[1])


def pick(flag, first, second):
    return jax.tree.map(lambda a, b: jnp.where(flag, a, b), first, second)


def packed(pair):
    rows = jnp.broadcast_to(pair[0][..., None, None], pair[0].shape + (8, pair[1].shape[-1]))
    return jnp.concatenate([pair[1], rows], axis=-2)


def unpacked(block):
    return (block[..., -8, 0], block[..., :-8, :])


def moved(tree, axis, pairs):
    if isinstance(tree, tuple):
        return unpacked(lax.ppermute(packed(tree), axis, pairs))
    return lax.ppermute(tree, axis, pairs)


def swap(tree, axis):
    return moved(tree, axis, [(0, 1), (1, 0)])


def shift(tree, axis, step):
    return moved(tree, axis, [(source, source - step) for source in range(step, lax.axis_size(axis))])


def suffix_scan(part):
    z_axis, pair_axis, core_axis = CTX
    core = lax.axis_index(core_axis)
    pair = lax.axis_index(pair_axis)
    plane = pair * 2 + core
    identity = jax.tree.map(lambda a: jnp.zeros_like(a) + jnp.asarray(1.0 if a.ndim == 1 else 0.0, a.dtype), part)
    other = swap(part, core_axis)
    pair_total = pick(core == 0, join(part, other), join(other, part))
    other_pair = swap(pair_total, pair_axis)
    total = pick(pair == 0, join(pair_total, other_pair), join(other_pair, pair_total))
    within = join(pick(core == 0, other, identity), pick(pair == 0, other_pair, identity))
    head = (
        lax.dynamic_index_in_dim(total[0], plane, 0, False),
        lax.dynamic_index_in_dim(total[1], plane, 0, False),
    )
    one = (jnp.ones_like(head[0]), jnp.zeros_like(head[1]))
    z = lax.axis_index(z_axis)
    count = lax.axis_size(z_axis)
    near = pick(z + 1 < count, shift(head, z_axis, 1), one)
    far = pick(z + 2 < count, shift(head, z_axis, 2), one)
    later = join(near, far)
    step = 2
    while step < count:
        later = pick(z + step < count, join(later, shift(later, z_axis, step)), later)
        step *= 2
    mine = later[1]
    theirs = swap(mine, core_axis)
    two = jnp.where(core == 0, jnp.stack([mine, theirs]), jnp.stack([theirs, mine]))
    two_other = swap(two, pair_axis)
    four = jnp.where(pair == 0, jnp.concatenate([two, two_other]), jnp.concatenate([two_other, two]))
    return within[1] + within[0][:, None, None] * four


def ssd_partials(ssm_input, gate_input, grad_out, shared_b, shared_c, log_decay, entry, block_len):
    head_count, length = log_decay.shape
    head_width = ssm_input.shape[1] // head_count
    span_count = length // block_len
    values_f = ssm_input.astype(jnp.float32).reshape(span_count, block_len, head_count, head_width)
    gates_f = gate_input.astype(jnp.float32).reshape(span_count, block_len, head_count, head_width)
    grad_f = grad_out.astype(jnp.float32).reshape(span_count, block_len, head_count, head_width)
    shared_bf = shared_b.astype(jnp.float32).reshape(span_count, block_len, shared_b.shape[1])
    shared_cf = shared_c.astype(jnp.float32).reshape(span_count, block_len, shared_c.shape[1])
    cumlog = jnp.cumsum(log_decay.reshape(head_count, span_count, block_len), axis=2)
    totals = cumlog[:, :, -1]
    causal = jnp.arange(block_len)[:, None] >= jnp.arange(block_len)[None, :]
    spread = cumlog[:, :, :, None] - cumlog[:, :, None, :]
    decay_mat = jnp.where(causal, jnp.exp(jnp.minimum(spread, 0.0)), 0.0)
    shared_c_blocks = shared_c.reshape(span_count, block_len, shared_c.shape[1])
    shared_b_blocks = shared_b.reshape(span_count, block_len, shared_b.shape[1])
    scores = jnp.einsum(
        "ktn,ksn->kts", shared_c_blocks, shared_b_blocks, preferred_element_type=jnp.float32
    )
    weighted = decay_mat * scores[None]
    to_end = jnp.exp(totals[:, :, None] - cumlog).transpose(1, 2, 0)
    from_start = jnp.exp(cumlog).transpose(1, 2, 0)
    scaled_x = values_f * to_end[..., None]
    local_states = jnp.einsum("ksn,kshp->khnp", shared_bf, scaled_x, precision=highest)
    span_decay = jnp.exp(totals).T

    def forward_step(running, inputs):
        decay_k, local_k = inputs
        return (decay_k[:, None, None] * running + local_k, running)

    _, entries = lax.scan(forward_step, entry, (span_decay, local_states))
    ssm_out = jnp.einsum("hkts,kshp->kthp", weighted, values_f, precision=highest)
    ssm_out = ssm_out + from_start[..., None] * jnp.einsum(
        "ktn,khnp->kthp", shared_cf, entries, precision=highest
    )
    gate_sig = jax.nn.sigmoid(gates_f)
    grad_y = grad_f * gates_f * gate_sig
    grad_z = grad_f * ssm_out * gate_sig * (1.0 + gates_f * (1.0 - gate_sig))
    products = decay_mat * jnp.einsum("kthp,kshp->hkts", grad_y, values_f, precision=highest)
    scaled_dy = grad_y * from_start[..., None]
    grad_c = jnp.einsum("hkts,ksn->ktn", products, shared_bf, precision=highest)
    grad_c = grad_c + jnp.einsum("kthp,khnp->ktn", scaled_dy, entries, precision=highest)
    grad_b = jnp.einsum("hkst,ksn->ktn", products, shared_cf, precision=highest)
    grad_x = jnp.einsum("hkst,kshp->kthp", weighted, grad_y, precision=highest)
    block_terms = jnp.einsum("ksn,kshp->khnp", shared_cf, scaled_dy, precision=highest)

    def backward_step(running, inputs):
        decay_k, term_k = inputs
        return (term_k + decay_k[:, None, None] * running, running)

    block_sum, later_sums = lax.scan(
        backward_step, jnp.zeros_like(entry), (span_decay, block_terms), reverse=True
    )
    block_log = jnp.sum(totals, axis=1)
    suffix = block_log[None, :] - jnp.cumsum(totals, axis=1).T
    grad_z_out = grad_z.reshape(length, head_count * head_width).astype(jnp.bfloat16)
    return (
        grad_z_out,
        grad_x,
        grad_b,
        grad_c,
        later_sums,
        suffix,
        to_end,
        scaled_x,
        shared_bf,
        block_sum,
        block_log,
    )


def finish_block(partials, incoming):
    (
        grad_z_out,
        grad_x,
        grad_b,
        grad_c,
        later_sums,
        suffix,
        to_end,
        scaled_x,
        shared_bf,
        block_sum,
        block_log,
    ) = partials
    carried = later_sums + jnp.exp(suffix)[:, :, None, None] * incoming[None]
    grad_x = grad_x + to_end[..., None] * jnp.einsum(
        "ktn,khnp->kthp", shared_bf, carried, precision=highest
    )
    grad_b = grad_b + jnp.einsum("kthp,khnp->ktn", scaled_x, carried, precision=highest)
    length = grad_z_out.shape[0]
    grad_x_out = grad_x.reshape(length, grad_z_out.shape[1]).astype(jnp.bfloat16)
    grad_bc = jnp.concatenate([grad_b.reshape(length, -1), grad_c.reshape(length, -1)], axis=1)
    return (grad_z_out, grad_x_out, grad_bc)


def times_rows(left, weights):
    return lax.dot_general(
        left, weights, (((1,), (1,)), ((), ())), preferred_element_type=jnp.float32
    )


def row_term(events, projected, norm_scale):
    return (
        lax.dot_general(
            events, projected, (((0,), (0,)), ((), ())), preferred_element_type=jnp.float32
        )
        * norm_scale
    )


def summed_over(part, axis, split):
    gathered = lax.all_to_all(part, axis, split, split, tiled=True)
    shape = gathered.shape
    pieces = shape[:split] + (lax.axis_size(axis), shape[split] // lax.axis_size(axis)) + shape[split + 1 :]
    return jnp.sum(gathered.astype(jnp.float32).reshape(pieces), axis=split)


def spread_sum(part, axis):
    count = lax.axis_size(axis)
    place = lax.axis_index(axis)
    chunks = part.reshape(part.shape[0], count, part.shape[1] // count).transpose(1, 0, 2)
    total = lax.dynamic_index_in_dim(chunks, place, 0, False).astype(jnp.float32)
    for step in range(1, count):
        piece = lax.dynamic_index_in_dim(chunks, (place - step) % count, 0, False)
        pairs = [(source, (source - step) % count) for source in range(count)]
        total = total + lax.ppermute(piece, axis, pairs).astype(jnp.float32)
    return total


def per_device(
    events,
    ssm_input,
    gate_input,
    grad_out,
    shared_b,
    shared_c,
    log_decay,
    entry_state,
    w_gate,
    w_value,
    w_shared,
):
    partials = ssd_partials(
        ssm_input, gate_input, grad_out, shared_b, shared_c, log_decay, entry_state[0], SPAN
    )
    block_sum = partials[9]
    block_log = partials[10]
    incoming = suffix_scan((jnp.exp(block_log), block_sum))
    grad_z, grad_x, grad_bc_part = finish_block(partials, incoming)
    grad_bc = summed_over(grad_bc_part, HEAD, 1).astype(jnp.bfloat16)
    input_part = (
        times_rows(grad_z, w_gate) + times_rows(grad_x, w_value) + times_rows(grad_bc, w_shared)
    )
    grad_input = spread_sum(input_part.astype(jnp.bfloat16), HEAD).astype(jnp.bfloat16)
    norm_scale = 1.0 / math.sqrt(events.shape[0] * lax.axis_size(CTX))
    head_cols = grad_z.shape[1]
    projected = jnp.concatenate([grad_z, grad_x, grad_bc], axis=1)
    rows = row_term(events, projected, norm_scale)
    sizes = [lax.axis_size(name) for name in CTX]
    rows = rows.reshape(*sizes, rows.shape[0] // math.prod(sizes), rows.shape[1])
    for level in reversed(range(len(CTX))):
        rows = summed_over(rows.astype(jnp.bfloat16), CTX[level], level)
    reduced = rows.reshape(rows.shape[-2], rows.shape[-1])
    grad_w_gate = reduced[:, :head_cols]
    grad_w_value = reduced[:, head_cols : 2 * head_cols]
    grad_w_shared = reduced[:, 2 * head_cols :]
    return (grad_input, grad_w_gate, grad_w_value, grad_w_shared)


CTX = ("z", "y_lo", "core")
HEAD = ("y_hi", "x")


def solution(mesh):
    ctx_size, head_size = mesh.devices.shape
    z_size = ctx_size // 4
    fine = jax.sharding.Mesh(
        mesh.devices.reshape(z_size, 2, 2, 2, head_size // 2),
        CTX + HEAD,
    )
    rows = P(CTX, None)
    both = P(CTX, HEAD)
    placed = (
        rows,
        both,
        both,
        both,
        rows,
        rows,
        P(HEAD, CTX),
        P(CTX, HEAD, None, None),
        P(None, HEAD),
        P(None, HEAD),
        P(None, HEAD),
    )
    return jax.shard_map(
        per_device,
        mesh=fine,
        in_specs=placed,
        out_specs=(both, both, both, both),
        check_vma=False,
    )
```

```python
import math

import jax
import jax.numpy as jnp
from jax import lax
from jax.sharding import PartitionSpec as P

SPAN = 256


highest = lax.Precision.HIGHEST


def join(near, far):
    return (near[0] * far[0], near[1] + near[0][..., None, None] * far[1])


def pick(flag, first, second):
    return jax.tree.map(lambda a, b: jnp.where(flag, a, b), first, second)


def packed(pair):
    rows = jnp.broadcast_to(pair[0][..., None, None], pair[0].shape + (8, pair[1].shape[-1]))
    return jnp.concatenate([pair[1], rows], axis=-2)


def unpacked(block):
    return (block[..., -8, 0], block[..., :-8, :])


def moved(tree, axis, pairs):
    if isinstance(tree, tuple):
        return unpacked(lax.ppermute(packed(tree), axis, pairs))
    return lax.ppermute(tree, axis, pairs)


def swap(tree, axis):
    return moved(tree, axis, [(0, 1), (1, 0)])


def shift(tree, axis, step):
    return moved(tree, axis, [(source, source - step) for source in range(step, lax.axis_size(axis))])


def suffix_scan(part):
    z_axis, pair_axis, core_axis = CTX
    core = lax.axis_index(core_axis)
    pair = lax.axis_index(pair_axis)
    plane = pair * 2 + core
    identity = jax.tree.map(lambda a: jnp.zeros_like(a) + jnp.asarray(1.0 if a.ndim == 1 else 0.0, a.dtype), part)
    other = swap(part, core_axis)
    pair_total = pick(core == 0, join(part, other), join(other, part))
    other_pair = swap(pair_total, pair_axis)
    total = pick(pair == 0, join(pair_total, other_pair), join(other_pair, pair_total))
    within = join(pick(core == 0, other, identity), pick(pair == 0, other_pair, identity))
    head = (
        lax.dynamic_index_in_dim(total[0], plane, 0, False),
        lax.dynamic_index_in_dim(total[1], plane, 0, False),
    )
    one = (jnp.ones_like(head[0]), jnp.zeros_like(head[1]))
    z = lax.axis_index(z_axis)
    count = lax.axis_size(z_axis)
    planes = unpacked(lax.all_gather(packed(head), z_axis))
    later = one
    for source in reversed(range(count)):
        later = pick(source > z, join((planes[0][source], planes[1][source]), later), later)
    mine = later[1]
    theirs = swap(mine, core_axis)
    two = jnp.where(core == 0, jnp.stack([mine, theirs]), jnp.stack([theirs, mine]))
    two_other = swap(two, pair_axis)
    four = jnp.where(pair == 0, jnp.concatenate([two, two_other]), jnp.concatenate([two_other, two]))
    return within[1] + within[0][:, None, None] * four


def ssd_partials(ssm_input, gate_input, grad_out, shared_b, shared_c, log_decay, entry, block_len):
    head_count, length = log_decay.shape
    head_width = ssm_input.shape[1] // head_count
    span_count = length // block_len
    values_f = ssm_input.astype(jnp.float32).reshape(span_count, block_len, head_count, head_width)
    gates_f = gate_input.astype(jnp.float32).reshape(span_count, block_len, head_count, head_width)
    grad_f = grad_out.astype(jnp.float32).reshape(span_count, block_len, head_count, head_width)
    shared_bf = shared_b.astype(jnp.float32).reshape(span_count, block_len, shared_b.shape[1])
    shared_cf = shared_c.astype(jnp.float32).reshape(span_count, block_len, shared_c.shape[1])
    cumlog = jnp.cumsum(log_decay.reshape(head_count, span_count, block_len), axis=2)
    totals = cumlog[:, :, -1]
    causal = jnp.arange(block_len)[:, None] >= jnp.arange(block_len)[None, :]
    spread = cumlog[:, :, :, None] - cumlog[:, :, None, :]
    decay_mat = jnp.where(causal, jnp.exp(jnp.minimum(spread, 0.0)), 0.0)
    shared_c_blocks = shared_c.reshape(span_count, block_len, shared_c.shape[1])
    shared_b_blocks = shared_b.reshape(span_count, block_len, shared_b.shape[1])
    scores = jnp.einsum(
        "ktn,ksn->kts", shared_c_blocks, shared_b_blocks, preferred_element_type=jnp.float32
    )
    weighted = decay_mat * scores[None]
    to_end = jnp.exp(totals[:, :, None] - cumlog).transpose(1, 2, 0)
    from_start = jnp.exp(cumlog).transpose(1, 2, 0)
    scaled_x = values_f * to_end[..., None]
    local_states = jnp.einsum("ksn,kshp->khnp", shared_bf, scaled_x, precision=highest)
    span_decay = jnp.exp(totals).T

    def forward_step(running, inputs):
        decay_k, local_k = inputs
        return (decay_k[:, None, None] * running + local_k, running)

    _, entries = lax.scan(forward_step, entry, (span_decay, local_states))
    ssm_out = jnp.einsum("hkts,kshp->kthp", weighted, values_f, precision=highest)
    ssm_out = ssm_out + from_start[..., None] * jnp.einsum(
        "ktn,khnp->kthp", shared_cf, entries, precision=highest
    )
    gate_sig = jax.nn.sigmoid(gates_f)
    grad_y = grad_f * gates_f * gate_sig
    grad_z = grad_f * ssm_out * gate_sig * (1.0 + gates_f * (1.0 - gate_sig))
    products = decay_mat * jnp.einsum("kthp,kshp->hkts", grad_y, values_f, precision=highest)
    scaled_dy = grad_y * from_start[..., None]
    grad_c = jnp.einsum("hkts,ksn->ktn", products, shared_bf, precision=highest)
    grad_c = grad_c + jnp.einsum("kthp,khnp->ktn", scaled_dy, entries, precision=highest)
    grad_b = jnp.einsum("hkst,ksn->ktn", products, shared_cf, precision=highest)
    grad_x = jnp.einsum("hkst,kshp->kthp", weighted, grad_y, precision=highest)
    block_terms = jnp.einsum("ksn,kshp->khnp", shared_cf, scaled_dy, precision=highest)

    def backward_step(running, inputs):
        decay_k, term_k = inputs
        return (term_k + decay_k[:, None, None] * running, running)

    block_sum, later_sums = lax.scan(
        backward_step, jnp.zeros_like(entry), (span_decay, block_terms), reverse=True
    )
    block_log = jnp.sum(totals, axis=1)
    suffix = block_log[None, :] - jnp.cumsum(totals, axis=1).T
    grad_z_out = grad_z.reshape(length, head_count * head_width).astype(jnp.bfloat16)
    return (
        grad_z_out,
        grad_x,
        grad_b,
        grad_c,
        later_sums,
        suffix,
        to_end,
        scaled_x,
        shared_bf,
        block_sum,
        block_log,
    )


def finish_block(partials, incoming):
    (
        grad_z_out,
        grad_x,
        grad_b,
        grad_c,
        later_sums,
        suffix,
        to_end,
        scaled_x,
        shared_bf,
        block_sum,
        block_log,
    ) = partials
    carried = later_sums + jnp.exp(suffix)[:, :, None, None] * incoming[None]
    grad_x = grad_x + to_end[..., None] * jnp.einsum(
        "ktn,khnp->kthp", shared_bf, carried, precision=highest
    )
    grad_b = grad_b + jnp.einsum("kthp,khnp->ktn", scaled_x, carried, precision=highest)
    length = grad_z_out.shape[0]
    grad_x_out = grad_x.reshape(length, grad_z_out.shape[1]).astype(jnp.bfloat16)
    grad_bc = jnp.concatenate([grad_b.reshape(length, -1), grad_c.reshape(length, -1)], axis=1)
    return (grad_z_out, grad_x_out, grad_bc)


def times_rows(left, weights):
    return lax.dot_general(
        left, weights, (((1,), (1,)), ((), ())), preferred_element_type=jnp.float32
    )


def row_term(events, projected, norm_scale):
    return (
        lax.dot_general(
            events, projected, (((0,), (0,)), ((), ())), preferred_element_type=jnp.float32
        )
        * norm_scale
    )


def summed_over(part, axis, split):
    gathered = lax.all_to_all(part, axis, split, split, tiled=True)
    shape = gathered.shape
    pieces = shape[:split] + (lax.axis_size(axis), shape[split] // lax.axis_size(axis)) + shape[split + 1 :]
    return jnp.sum(gathered.astype(jnp.float32).reshape(pieces), axis=split)


def spread_sum(part, axis):
    count = lax.axis_size(axis)
    place = lax.axis_index(axis)
    chunks = part.reshape(part.shape[0], count, part.shape[1] // count).transpose(1, 0, 2)
    total = lax.dynamic_index_in_dim(chunks, place, 0, False).astype(jnp.float32)
    for step in range(1, count):
        piece = lax.dynamic_index_in_dim(chunks, (place - step) % count, 0, False)
        pairs = [(source, (source - step) % count) for source in range(count)]
        total = total + lax.ppermute(piece, axis, pairs).astype(jnp.float32)
    return total


def per_device(
    events,
    ssm_input,
    gate_input,
    grad_out,
    shared_b,
    shared_c,
    log_decay,
    entry_state,
    w_gate,
    w_value,
    w_shared,
):
    partials = ssd_partials(
        ssm_input, gate_input, grad_out, shared_b, shared_c, log_decay, entry_state[0], SPAN
    )
    block_sum = partials[9]
    block_log = partials[10]
    incoming = suffix_scan((jnp.exp(block_log), block_sum))
    grad_z, grad_x, grad_bc_part = finish_block(partials, incoming)
    grad_bc = summed_over(grad_bc_part, HEAD, 1).astype(jnp.bfloat16)
    input_part = (
        times_rows(grad_z, w_gate) + times_rows(grad_x, w_value) + times_rows(grad_bc, w_shared)
    )
    grad_input = spread_sum(input_part.astype(jnp.bfloat16), HEAD).astype(jnp.bfloat16)
    norm_scale = 1.0 / math.sqrt(events.shape[0] * lax.axis_size(CTX))
    head_cols = grad_z.shape[1]
    projected = jnp.concatenate([grad_z, grad_x, grad_bc], axis=1)
    rows = row_term(events, projected, norm_scale)
    sizes = [lax.axis_size(name) for name in CTX]
    rows = rows.reshape(*sizes, rows.shape[0] // math.prod(sizes), rows.shape[1])
    for level in reversed(range(len(CTX))):
        rows = summed_over(rows.astype(jnp.bfloat16), CTX[level], level)
    reduced = rows.reshape(rows.shape[-2], rows.shape[-1])
    grad_w_gate = reduced[:, :head_cols]
    grad_w_value = reduced[:, head_cols : 2 * head_cols]
    grad_w_shared = reduced[:, 2 * head_cols :]
    return (grad_input, grad_w_gate, grad_w_value, grad_w_shared)


CTX = ("z", "y_lo", "core")
HEAD = ("y_hi", "x")


def solution(mesh):
    ctx_size, head_size = mesh.devices.shape
    z_size = ctx_size // 4
    fine = jax.sharding.Mesh(
        mesh.devices.reshape(z_size, 2, 2, 2, head_size // 2),
        CTX + HEAD,
    )
    rows = P(CTX, None)
    both = P(CTX, HEAD)
    placed = (
        rows,
        both,
        both,
        both,
        rows,
        rows,
        P(HEAD, CTX),
        P(CTX, HEAD, None, None),
        P(None, HEAD),
        P(None, HEAD),
        P(None, HEAD),
    )
    return jax.shard_map(
        per_device,
        mesh=fine,
        in_specs=placed,
        out_specs=(both, both, both, both),
        check_vma=False,
    )
```

```python
import math

import jax
import jax.numpy as jnp
from jax import lax
from jax.sharding import PartitionSpec as P

SPAN = 256


highest = lax.Precision.HIGHEST


def join(near, far):
    return (near[0] * far[0], near[1] + near[0][..., None, None] * far[1])


def pick(flag, first, second):
    return jax.tree.map(lambda a, b: jnp.where(flag, a, b), first, second)


def swap(tree, axis):
    return jax.tree.map(lambda a: lax.ppermute(a, axis, [(0, 1), (1, 0)]), tree)


def shift(tree, axis, step):
    pairs = [(source, source - step) for source in range(step, lax.axis_size(axis))]
    return jax.tree.map(lambda a: lax.ppermute(a, axis, pairs), tree)


def suffix_scan(part, tied):
    z_axis, pair_axis, core_axis = CTX
    core = lax.axis_index(core_axis)
    pair = lax.axis_index(pair_axis)
    plane = pair * 2 + core
    identity = jax.tree.map(lambda a: jnp.zeros_like(a) + jnp.asarray(1.0 if a.ndim == 1 else 0.0, a.dtype), part)
    other = swap(part, core_axis)
    pair_total = pick(core == 0, join(part, other), join(other, part))
    other_pair = swap(pair_total, pair_axis)
    total = pick(pair == 0, join(pair_total, other_pair), join(other_pair, pair_total))
    within = join(pick(core == 0, other, identity), pick(pair == 0, other_pair, identity))
    head = (
        lax.dynamic_index_in_dim(total[0], plane, 0, False),
        lax.dynamic_index_in_dim(total[1], plane, 0, False),
    )
    one = (jnp.ones_like(head[0]), jnp.zeros_like(head[1]))
    z = lax.axis_index(z_axis)
    count = lax.axis_size(z_axis)
    near = pick(z + 1 < count, shift(head, z_axis, 1), one)
    far = pick(z + 2 < count, shift(head, z_axis, 2), one)
    later = join(near, far)
    step = 2
    while step < count:
        later = pick(z + step < count, join(later, shift(later, z_axis, step)), later)
        step *= 2
    mine, tied = lax.optimization_barrier((later[1], tied))
    theirs = swap(mine, core_axis)
    two = jnp.where(core == 0, jnp.stack([mine, theirs]), jnp.stack([theirs, mine]))
    two_other = swap(two, pair_axis)
    four = jnp.where(pair == 0, jnp.concatenate([two, two_other]), jnp.concatenate([two_other, two]))
    return within[1] + within[0][:, None, None] * four, tied


def ssd_partials(ssm_input, gate_input, grad_out, shared_b, shared_c, log_decay, entry, block_len):
    head_count, length = log_decay.shape
    head_width = ssm_input.shape[1] // head_count
    span_count = length // block_len
    values_f = ssm_input.astype(jnp.float32).reshape(span_count, block_len, head_count, head_width)
    gates_f = gate_input.astype(jnp.float32).reshape(span_count, block_len, head_count, head_width)
    grad_f = grad_out.astype(jnp.float32).reshape(span_count, block_len, head_count, head_width)
    shared_bf = shared_b.astype(jnp.float32).reshape(span_count, block_len, shared_b.shape[1])
    shared_cf = shared_c.astype(jnp.float32).reshape(span_count, block_len, shared_c.shape[1])
    cumlog = jnp.cumsum(log_decay.reshape(head_count, span_count, block_len), axis=2)
    totals = cumlog[:, :, -1]
    causal = jnp.arange(block_len)[:, None] >= jnp.arange(block_len)[None, :]
    spread = cumlog[:, :, :, None] - cumlog[:, :, None, :]
    decay_mat = jnp.where(causal, jnp.exp(jnp.minimum(spread, 0.0)), 0.0)
    shared_c_blocks = shared_c.reshape(span_count, block_len, shared_c.shape[1])
    shared_b_blocks = shared_b.reshape(span_count, block_len, shared_b.shape[1])
    scores = jnp.einsum(
        "ktn,ksn->kts", shared_c_blocks, shared_b_blocks, preferred_element_type=jnp.float32
    )
    weighted = decay_mat * scores[None]
    to_end = jnp.exp(totals[:, :, None] - cumlog).transpose(1, 2, 0)
    from_start = jnp.exp(cumlog).transpose(1, 2, 0)
    scaled_x = values_f * to_end[..., None]
    local_states = jnp.einsum("ksn,kshp->khnp", shared_bf, scaled_x, precision=highest)
    span_decay = jnp.exp(totals).T

    def forward_step(running, inputs):
        decay_k, local_k = inputs
        return (decay_k[:, None, None] * running + local_k, running)

    _, entries = lax.scan(forward_step, entry, (span_decay, local_states))
    ssm_out = jnp.einsum("hkts,kshp->kthp", weighted, values_f, precision=highest)
    ssm_out = ssm_out + from_start[..., None] * jnp.einsum(
        "ktn,khnp->kthp", shared_cf, entries, precision=highest
    )
    gate_sig = jax.nn.sigmoid(gates_f)
    grad_y = grad_f * gates_f * gate_sig
    grad_z = grad_f * ssm_out * gate_sig * (1.0 + gates_f * (1.0 - gate_sig))
    products = decay_mat * jnp.einsum("kthp,kshp->hkts", grad_y, values_f, precision=highest)
    scaled_dy = grad_y * from_start[..., None]
    grad_c = jnp.einsum("hkts,ksn->ktn", products, shared_bf, precision=highest)
    grad_c = grad_c + jnp.einsum("kthp,khnp->ktn", scaled_dy, entries, precision=highest)
    grad_b = jnp.einsum("hkst,ksn->ktn", products, shared_cf, precision=highest)
    grad_x = jnp.einsum("hkst,kshp->kthp", weighted, grad_y, precision=highest)
    block_terms = jnp.einsum("ksn,kshp->khnp", shared_cf, scaled_dy, precision=highest)

    def backward_step(running, inputs):
        decay_k, term_k = inputs
        return (term_k + decay_k[:, None, None] * running, running)

    block_sum, later_sums = lax.scan(
        backward_step, jnp.zeros_like(entry), (span_decay, block_terms), reverse=True
    )
    block_log = jnp.sum(totals, axis=1)
    suffix = block_log[None, :] - jnp.cumsum(totals, axis=1).T
    grad_z_out = grad_z.reshape(length, head_count * head_width).astype(jnp.bfloat16)
    return (
        grad_z_out,
        grad_x,
        grad_b,
        grad_c,
        later_sums,
        suffix,
        to_end,
        scaled_x,
        shared_bf,
        block_sum,
        block_log,
    )


def finish_block(partials, incoming):
    (
        grad_z_out,
        grad_x,
        grad_b,
        grad_c,
        later_sums,
        suffix,
        to_end,
        scaled_x,
        shared_bf,
        block_sum,
        block_log,
    ) = partials
    carried = later_sums + jnp.exp(suffix)[:, :, None, None] * incoming[None]
    grad_x = grad_x + to_end[..., None] * jnp.einsum(
        "ktn,khnp->kthp", shared_bf, carried, precision=highest
    )
    grad_b = grad_b + jnp.einsum("kthp,khnp->ktn", scaled_x, carried, precision=highest)
    length = grad_z_out.shape[0]
    grad_x_out = grad_x.reshape(length, grad_z_out.shape[1]).astype(jnp.bfloat16)
    grad_bc = jnp.concatenate([grad_b.reshape(length, -1), grad_c.reshape(length, -1)], axis=1)
    return (grad_z_out, grad_x_out, grad_bc)


def times_rows(left, weights):
    return lax.dot_general(
        left, weights, (((1,), (1,)), ((), ())), preferred_element_type=jnp.float32
    )


def row_term(events, projected, norm_scale):
    return (
        lax.dot_general(
            events, projected, (((0,), (0,)), ((), ())), preferred_element_type=jnp.float32
        )
        * norm_scale
    )


def summed_over(part, axis, split):
    gathered = lax.all_to_all(part, axis, split, split, tiled=True)
    shape = gathered.shape
    pieces = shape[:split] + (lax.axis_size(axis), shape[split] // lax.axis_size(axis)) + shape[split + 1 :]
    return jnp.sum(gathered.astype(jnp.float32).reshape(pieces), axis=split)


def spread_sum(part, axis):
    count = lax.axis_size(axis)
    place = lax.axis_index(axis)
    chunks = part.reshape(part.shape[0], count, part.shape[1] // count).transpose(1, 0, 2)
    total = lax.dynamic_index_in_dim(chunks, place, 0, False).astype(jnp.float32)
    for step in range(1, count):
        piece = lax.dynamic_index_in_dim(chunks, (place - step) % count, 0, False)
        pairs = [(source, (source - step) % count) for source in range(count)]
        total = total + lax.ppermute(piece, axis, pairs).astype(jnp.float32)
    return total


def swap_sum(rows, axis, dim):
    place = lax.axis_index(axis)
    own = lax.dynamic_index_in_dim(rows, place, dim, True)
    other = lax.dynamic_index_in_dim(rows, 1 - place, dim, True)
    return own + swap(other.astype(jnp.bfloat16), axis).astype(jnp.float32)


def reduce_rows(rows, paired):
    sizes = [lax.axis_size(name) for name in CTX]
    rows = rows.reshape(*sizes, rows.shape[0] // math.prod(sizes), rows.shape[1])
    for level in reversed(range(len(CTX))):
        if paired and level > 0:
            rows = swap_sum(rows, CTX[level], level)
        else:
            rows = summed_over(rows.astype(jnp.bfloat16), CTX[level], level)
    return rows.reshape(rows.shape[-2], rows.shape[-1])


def per_device(
    events,
    ssm_input,
    gate_input,
    grad_out,
    shared_b,
    shared_c,
    log_decay,
    entry_state,
    w_gate,
    w_value,
    w_shared,
):
    partials = ssd_partials(
        ssm_input, gate_input, grad_out, shared_b, shared_c, log_decay, entry_state[0], SPAN
    )
    block_sum = partials[9]
    block_log = partials[10]
    norm_scale = 1.0 / math.sqrt(events.shape[0] * lax.axis_size(CTX))
    gate_rows = reduce_rows(row_term(events, partials[0], norm_scale), True)
    incoming, gate_rows = suffix_scan((jnp.exp(block_log), block_sum), gate_rows)
    grad_z, grad_x, grad_bc_part = finish_block(partials, incoming)
    grad_bc = summed_over(grad_bc_part, HEAD, 1).astype(jnp.bfloat16)
    input_part = (
        times_rows(grad_z, w_gate) + times_rows(grad_x, w_value) + times_rows(grad_bc, w_shared)
    )
    grad_input = spread_sum(input_part.astype(jnp.bfloat16), HEAD).astype(jnp.bfloat16)
    head_cols = grad_z.shape[1]
    rest = jnp.concatenate([grad_x, grad_bc], axis=1)
    rest_rows = reduce_rows(row_term(events, rest, norm_scale), False)
    grad_w_gate = gate_rows
    grad_w_value = rest_rows[:, :head_cols]
    grad_w_shared = rest_rows[:, head_cols:]
    return (grad_input, grad_w_gate, grad_w_value, grad_w_shared)


CTX = ("z", "y_lo", "core")
HEAD = ("y_hi", "x")


def solution(mesh):
    ctx_size, head_size = mesh.devices.shape
    z_size = ctx_size // 4
    fine = jax.sharding.Mesh(
        mesh.devices.reshape(z_size, 2, 2, 2, head_size // 2),
        CTX + HEAD,
    )
    rows = P(CTX, None)
    both = P(CTX, HEAD)
    placed = (
        rows,
        both,
        both,
        both,
        rows,
        rows,
        P(HEAD, CTX),
        P(CTX, HEAD, None, None),
        P(None, HEAD),
        P(None, HEAD),
        P(None, HEAD),
    )
    return jax.shard_map(
        per_device,
        mesh=fine,
        in_specs=placed,
        out_specs=(both, both, both, both),
        check_vma=False,
    )
```

```python
import math

import jax
import jax.numpy as jnp
from jax import lax
from jax.sharding import PartitionSpec as P

SPAN = 256


highest = lax.Precision.HIGHEST


def join(near, far):
    return (near[0] * far[0], near[1] + near[0][..., None, None] * far[1])


def pick(flag, first, second):
    return jax.tree.map(lambda a, b: jnp.where(flag, a, b), first, second)


def swap(tree, axis):
    return jax.tree.map(lambda a: lax.ppermute(a, axis, [(0, 1), (1, 0)]), tree)


def shift(tree, axis, step):
    pairs = [(source, source - step) for source in range(step, lax.axis_size(axis))]
    return jax.tree.map(lambda a: lax.ppermute(a, axis, pairs), tree)


def suffix_scan(part):
    z_axis, pair_axis, core_axis = CTX
    core = lax.axis_index(core_axis)
    pair = lax.axis_index(pair_axis)
    plane = pair * 2 + core
    identity = jax.tree.map(lambda a: jnp.zeros_like(a) + jnp.asarray(1.0 if a.ndim == 1 else 0.0, a.dtype), part)
    other = swap(part, core_axis)
    pair_total = pick(core == 0, join(part, other), join(other, part))
    other_pair = swap(pair_total, pair_axis)
    total = pick(pair == 0, join(pair_total, other_pair), join(other_pair, pair_total))
    within = join(pick(core == 0, other, identity), pick(pair == 0, other_pair, identity))
    head = (
        lax.dynamic_index_in_dim(total[0], plane, 0, False),
        lax.dynamic_index_in_dim(total[1], plane, 0, False),
    )
    one = (jnp.ones_like(head[0]), jnp.zeros_like(head[1]))
    z = lax.axis_index(z_axis)
    count = lax.axis_size(z_axis)
    near = pick(z + 1 < count, shift(head, z_axis, 1), one)
    far = pick(z + 2 < count, shift(head, z_axis, 2), one)
    later = join(near, far)
    step = 2
    while step < count:
        later = pick(z + step < count, join(later, shift(later, z_axis, step)), later)
        step *= 2
    mine = later[1]
    theirs = swap(mine, core_axis)
    two = jnp.where(core == 0, jnp.stack([mine, theirs]), jnp.stack([theirs, mine]))
    two_other = swap(two, pair_axis)
    four = jnp.where(pair == 0, jnp.concatenate([two, two_other]), jnp.concatenate([two_other, two]))
    return within[1] + within[0][:, None, None] * four


def ssd_partials(ssm_input, gate_input, grad_out, shared_b, shared_c, log_decay, entry, block_len):
    head_count, length = log_decay.shape
    head_width = ssm_input.shape[1] // head_count
    span_count = length // block_len
    values_f = ssm_input.astype(jnp.float32).reshape(span_count, block_len, head_count, head_width)
    gates_f = gate_input.astype(jnp.float32).reshape(span_count, block_len, head_count, head_width)
    grad_f = grad_out.astype(jnp.float32).reshape(span_count, block_len, head_count, head_width)
    shared_bf = shared_b.astype(jnp.float32).reshape(span_count, block_len, shared_b.shape[1])
    shared_cf = shared_c.astype(jnp.float32).reshape(span_count, block_len, shared_c.shape[1])
    cumlog = jnp.cumsum(log_decay.reshape(head_count, span_count, block_len), axis=2)
    totals = cumlog[:, :, -1]
    causal = jnp.arange(block_len)[:, None] >= jnp.arange(block_len)[None, :]
    spread = cumlog[:, :, :, None] - cumlog[:, :, None, :]
    decay_mat = jnp.where(causal, jnp.exp(jnp.minimum(spread, 0.0)), 0.0)
    shared_c_blocks = shared_c.reshape(span_count, block_len, shared_c.shape[1])
    shared_b_blocks = shared_b.reshape(span_count, block_len, shared_b.shape[1])
    scores = jnp.einsum(
        "ktn,ksn->kts", shared_c_blocks, shared_b_blocks, preferred_element_type=jnp.float32
    )
    weighted = decay_mat * scores[None]
    to_end = jnp.exp(totals[:, :, None] - cumlog).transpose(1, 2, 0)
    from_start = jnp.exp(cumlog).transpose(1, 2, 0)
    scaled_x = values_f * to_end[..., None]
    local_states = jnp.einsum("ksn,kshp->khnp", shared_bf, scaled_x, precision=highest)
    span_decay = jnp.exp(totals).T

    def forward_step(running, inputs):
        decay_k, local_k = inputs
        return (decay_k[:, None, None] * running + local_k, running)

    _, entries = lax.scan(forward_step, entry, (span_decay, local_states))
    ssm_out = jnp.einsum("hkts,kshp->kthp", weighted, values_f, precision=highest)
    ssm_out = ssm_out + from_start[..., None] * jnp.einsum(
        "ktn,khnp->kthp", shared_cf, entries, precision=highest
    )
    gate_sig = jax.nn.sigmoid(gates_f)
    grad_y = grad_f * gates_f * gate_sig
    grad_z = grad_f * ssm_out * gate_sig * (1.0 + gates_f * (1.0 - gate_sig))
    products = decay_mat * jnp.einsum("kthp,kshp->hkts", grad_y, values_f, precision=highest)
    scaled_dy = grad_y * from_start[..., None]
    grad_c = jnp.einsum("hkts,ksn->ktn", products, shared_bf, precision=highest)
    grad_c = grad_c + jnp.einsum("kthp,khnp->ktn", scaled_dy, entries, precision=highest)
    grad_b = jnp.einsum("hkst,ksn->ktn", products, shared_cf, precision=highest)
    grad_x = jnp.einsum("hkst,kshp->kthp", weighted, grad_y, precision=highest)
    block_terms = jnp.einsum("ksn,kshp->khnp", shared_cf, scaled_dy, precision=highest)

    def backward_step(running, inputs):
        decay_k, term_k = inputs
        return (term_k + decay_k[:, None, None] * running, running)

    block_sum, later_sums = lax.scan(
        backward_step, jnp.zeros_like(entry), (span_decay, block_terms), reverse=True
    )
    block_log = jnp.sum(totals, axis=1)
    suffix = block_log[None, :] - jnp.cumsum(totals, axis=1).T
    grad_z_out = grad_z.reshape(length, head_count * head_width).astype(jnp.bfloat16)
    return (
        grad_z_out,
        grad_x,
        grad_b,
        grad_c,
        later_sums,
        suffix,
        to_end,
        scaled_x,
        shared_bf,
        block_sum,
        block_log,
    )


def finish_block(partials, incoming):
    (
        grad_z_out,
        grad_x,
        grad_b,
        grad_c,
        later_sums,
        suffix,
        to_end,
        scaled_x,
        shared_bf,
        block_sum,
        block_log,
    ) = partials
    carried = later_sums + jnp.exp(suffix)[:, :, None, None] * incoming[None]
    grad_x = grad_x + to_end[..., None] * jnp.einsum(
        "ktn,khnp->kthp", shared_bf, carried, precision=highest
    )
    grad_b = grad_b + jnp.einsum("kthp,khnp->ktn", scaled_x, carried, precision=highest)
    length = grad_z_out.shape[0]
    grad_x_out = grad_x.reshape(length, grad_z_out.shape[1]).astype(jnp.bfloat16)
    grad_bc = jnp.concatenate([grad_b.reshape(length, -1), grad_c.reshape(length, -1)], axis=1)
    return (grad_z_out, grad_x_out, grad_bc)


def times_rows(left, weights):
    return lax.dot_general(
        left, weights, (((1,), (1,)), ((), ())), preferred_element_type=jnp.float32
    )


def row_term(events, projected, norm_scale):
    return (
        lax.dot_general(
            events, projected, (((0,), (0,)), ((), ())), preferred_element_type=jnp.float32
        )
        * norm_scale
    )


def summed_over(part, axis, split):
    gathered = lax.all_to_all(part, axis, split, split, tiled=True)
    shape = gathered.shape
    pieces = shape[:split] + (lax.axis_size(axis), shape[split] // lax.axis_size(axis)) + shape[split + 1 :]
    return jnp.sum(gathered.astype(jnp.float32).reshape(pieces), axis=split)


def spread_sum(part, axis):
    count = lax.axis_size(axis)
    place = lax.axis_index(axis)
    chunks = part.reshape(part.shape[0], count, part.shape[1] // count).transpose(1, 0, 2)
    total = lax.dynamic_index_in_dim(chunks, place, 0, False).astype(jnp.float32)
    for step in range(1, count):
        piece = lax.dynamic_index_in_dim(chunks, (place - step) % count, 0, False)
        pairs = [(source, (source - step) % count) for source in range(count)]
        total = total + lax.ppermute(piece, axis, pairs).astype(jnp.float32)
    return total


def swap_sum(rows, axis, dim):
    place = lax.axis_index(axis)
    own = lax.dynamic_index_in_dim(rows, place, dim, True)
    other = lax.dynamic_index_in_dim(rows, 1 - place, dim, True)
    return own + swap(other.astype(jnp.bfloat16), axis).astype(jnp.float32)


def per_device(
    events,
    ssm_input,
    gate_input,
    grad_out,
    shared_b,
    shared_c,
    log_decay,
    entry_state,
    w_gate,
    w_value,
    w_shared,
):
    partials = ssd_partials(
        ssm_input, gate_input, grad_out, shared_b, shared_c, log_decay, entry_state[0], SPAN
    )
    block_sum = partials[9]
    block_log = partials[10]
    incoming = suffix_scan((jnp.exp(block_log), block_sum))
    grad_z, grad_x, grad_bc_part = finish_block(partials, incoming)
    grad_bc = summed_over(grad_bc_part, HEAD, 1).astype(jnp.bfloat16)
    input_part = (
        times_rows(grad_z, w_gate) + times_rows(grad_x, w_value) + times_rows(grad_bc, w_shared)
    )
    grad_input = spread_sum(input_part.astype(jnp.bfloat16), HEAD).astype(jnp.bfloat16)
    norm_scale = 1.0 / math.sqrt(events.shape[0] * lax.axis_size(CTX))
    head_cols = grad_z.shape[1]
    projected = jnp.concatenate([grad_z, grad_x, grad_bc], axis=1)
    rows = row_term(events, projected, norm_scale)
    sizes = [lax.axis_size(name) for name in CTX]
    rows = rows.reshape(*sizes, rows.shape[0] // math.prod(sizes), rows.shape[1])
    for level in reversed(range(len(CTX))):
        if level > 0:
            rows = swap_sum(rows, CTX[level], level)
        else:
            rows = summed_over(rows.astype(jnp.bfloat16), CTX[level], level)
    reduced = rows.reshape(rows.shape[-2], rows.shape[-1])
    grad_w_gate = reduced[:, :head_cols]
    grad_w_value = reduced[:, head_cols : 2 * head_cols]
    grad_w_shared = reduced[:, 2 * head_cols :]
    return (grad_input, grad_w_gate, grad_w_value, grad_w_shared)


CTX = ("z", "y_lo", "core")
HEAD = ("y_hi", "x")


def solution(mesh):
    ctx_size, head_size = mesh.devices.shape
    z_size = ctx_size // 4
    fine = jax.sharding.Mesh(
        mesh.devices.reshape(z_size, 2, 2, 2, head_size // 2),
        CTX + HEAD,
    )
    rows = P(CTX, None)
    both = P(CTX, HEAD)
    placed = (
        rows,
        both,
        both,
        both,
        rows,
        rows,
        P(HEAD, CTX),
        P(CTX, HEAD, None, None),
        P(None, HEAD),
        P(None, HEAD),
        P(None, HEAD),
    )
    return jax.shard_map(
        per_device,
        mesh=fine,
        in_specs=placed,
        out_specs=(both, both, both, both),
        check_vma=False,
    )
```

```python
import math

import jax
import jax.numpy as jnp
from jax import lax
from jax.sharding import PartitionSpec as P

SPAN = 256


highest = lax.Precision.HIGHEST


def join(near, far):
    return (near[0] * far[0], near[1] + near[0][..., None, None] * far[1])


def pick(flag, first, second):
    return jax.tree.map(lambda a, b: jnp.where(flag, a, b), first, second)


def swap(tree, axis):
    return jax.tree.map(lambda a: lax.ppermute(a, axis, [(0, 1), (1, 0)]), tree)


def shift(tree, axis, step):
    pairs = [(source, source - step) for source in range(step, lax.axis_size(axis))]
    return jax.tree.map(lambda a: lax.ppermute(a, axis, pairs), tree)


def suffix_scan(part):
    z_axis, pair_axis, core_axis = CTX
    core = lax.axis_index(core_axis)
    pair = lax.axis_index(pair_axis)
    plane = pair * 2 + core
    identity = jax.tree.map(lambda a: jnp.zeros_like(a) + jnp.asarray(1.0 if a.ndim == 1 else 0.0, a.dtype), part)
    other = swap(part, core_axis)
    pair_total = pick(core == 0, join(part, other), join(other, part))
    other_pair = swap(pair_total, pair_axis)
    total = pick(pair == 0, join(pair_total, other_pair), join(other_pair, pair_total))
    within = join(pick(core == 0, other, identity), pick(pair == 0, other_pair, identity))
    head = (
        lax.dynamic_index_in_dim(total[0], plane, 0, False),
        lax.dynamic_index_in_dim(total[1], plane, 0, False),
    )
    one = (jnp.ones_like(head[0]), jnp.zeros_like(head[1]))
    z = lax.axis_index(z_axis)
    count = lax.axis_size(z_axis)
    near = pick(z + 1 < count, shift(head, z_axis, 1), one)
    far = pick(z + 2 < count, shift(head, z_axis, 2), one)
    later = join(near, far)
    step = 2
    while step < count:
        later = pick(z + step < count, join(later, shift(later, z_axis, step)), later)
        step *= 2
    mine = later[1]
    theirs = swap(mine, core_axis)
    two = jnp.where(core == 0, jnp.stack([mine, theirs]), jnp.stack([theirs, mine]))
    two_other = swap(two, pair_axis)
    four = jnp.where(pair == 0, jnp.concatenate([two, two_other]), jnp.concatenate([two_other, two]))
    return within[1] + within[0][:, None, None] * four


def ssd_partials(ssm_input, gate_input, grad_out, shared_b, shared_c, log_decay, entry, block_len):
    head_count, length = log_decay.shape
    head_width = ssm_input.shape[1] // head_count
    span_count = length // block_len
    values_f = ssm_input.astype(jnp.float32).reshape(span_count, block_len, head_count, head_width)
    gates_f = gate_input.astype(jnp.float32).reshape(span_count, block_len, head_count, head_width)
    grad_f = grad_out.astype(jnp.float32).reshape(span_count, block_len, head_count, head_width)
    shared_bf = shared_b.astype(jnp.float32).reshape(span_count, block_len, shared_b.shape[1])
    shared_cf = shared_c.astype(jnp.float32).reshape(span_count, block_len, shared_c.shape[1])
    cumlog = jnp.cumsum(log_decay.reshape(head_count, span_count, block_len), axis=2)
    totals = cumlog[:, :, -1]
    causal = jnp.arange(block_len)[:, None] >= jnp.arange(block_len)[None, :]
    spread = cumlog[:, :, :, None] - cumlog[:, :, None, :]
    decay_mat = jnp.where(causal, jnp.exp(jnp.minimum(spread, 0.0)), 0.0)
    shared_c_blocks = shared_c.reshape(span_count, block_len, shared_c.shape[1])
    shared_b_blocks = shared_b.reshape(span_count, block_len, shared_b.shape[1])
    scores = jnp.einsum(
        "ktn,ksn->kts", shared_c_blocks, shared_b_blocks, preferred_element_type=jnp.float32
    )
    weighted = decay_mat * scores[None]
    to_end = jnp.exp(totals[:, :, None] - cumlog).transpose(1, 2, 0)
    from_start = jnp.exp(cumlog).transpose(1, 2, 0)
    scaled_x = values_f * to_end[..., None]
    local_states = jnp.einsum("ksn,kshp->khnp", shared_bf, scaled_x, precision=highest)
    span_decay = jnp.exp(totals).T

    def forward_step(running, inputs):
        decay_k, local_k = inputs
        return (decay_k[:, None, None] * running + local_k, running)

    _, entries = lax.scan(forward_step, entry, (span_decay, local_states))
    ssm_out = jnp.einsum("hkts,kshp->kthp", weighted, values_f, precision=highest)
    ssm_out = ssm_out + from_start[..., None] * jnp.einsum(
        "ktn,khnp->kthp", shared_cf, entries, precision=highest
    )
    gate_sig = jax.nn.sigmoid(gates_f)
    grad_y = grad_f * gates_f * gate_sig
    grad_z = grad_f * ssm_out * gate_sig * (1.0 + gates_f * (1.0 - gate_sig))
    products = decay_mat * jnp.einsum("kthp,kshp->hkts", grad_y, values_f, precision=highest)
    scaled_dy = grad_y * from_start[..., None]
    grad_c = jnp.einsum("hkts,ksn->ktn", products, shared_bf, precision=highest)
    grad_c = grad_c + jnp.einsum("kthp,khnp->ktn", scaled_dy, entries, precision=highest)
    grad_b = jnp.einsum("hkst,ksn->ktn", products, shared_cf, precision=highest)
    grad_x = jnp.einsum("hkst,kshp->kthp", weighted, grad_y, precision=highest)
    block_terms = jnp.einsum("ksn,kshp->khnp", shared_cf, scaled_dy, precision=highest)

    def backward_step(running, inputs):
        decay_k, term_k = inputs
        return (term_k + decay_k[:, None, None] * running, running)

    block_sum, later_sums = lax.scan(
        backward_step, jnp.zeros_like(entry), (span_decay, block_terms), reverse=True
    )
    block_log = jnp.sum(totals, axis=1)
    suffix = block_log[None, :] - jnp.cumsum(totals, axis=1).T
    grad_z_out = grad_z.reshape(length, head_count * head_width).astype(jnp.bfloat16)
    return (
        grad_z_out,
        grad_x,
        grad_b,
        grad_c,
        later_sums,
        suffix,
        to_end,
        scaled_x,
        shared_bf,
        block_sum,
        block_log,
    )


def finish_block(partials, incoming):
    (
        grad_z_out,
        grad_x,
        grad_b,
        grad_c,
        later_sums,
        suffix,
        to_end,
        scaled_x,
        shared_bf,
        block_sum,
        block_log,
    ) = partials
    carried = later_sums + jnp.exp(suffix)[:, :, None, None] * incoming[None]
    grad_x = grad_x + to_end[..., None] * jnp.einsum(
        "ktn,khnp->kthp", shared_bf, carried, precision=highest
    )
    grad_b = grad_b + jnp.einsum("kthp,khnp->ktn", scaled_x, carried, precision=highest)
    length = grad_z_out.shape[0]
    grad_x_out = grad_x.reshape(length, grad_z_out.shape[1]).astype(jnp.bfloat16)
    grad_bc = jnp.concatenate([grad_b.reshape(length, -1), grad_c.reshape(length, -1)], axis=1)
    return (grad_z_out, grad_x_out, grad_bc)


def times_rows(left, weights):
    return lax.dot_general(
        left, weights, (((1,), (1,)), ((), ())), preferred_element_type=jnp.float32
    )


def row_term(events, projected, norm_scale):
    return (
        lax.dot_general(
            events, projected, (((0,), (0,)), ((), ())), preferred_element_type=jnp.float32
        )
        * norm_scale
    )


def summed_over(part, axis, split):
    gathered = lax.all_to_all(part, axis, split, split, tiled=True)
    shape = gathered.shape
    pieces = shape[:split] + (lax.axis_size(axis), shape[split] // lax.axis_size(axis)) + shape[split + 1 :]
    return jnp.sum(gathered.astype(jnp.float32).reshape(pieces), axis=split)


def spread_sum(part, axis):
    count = lax.axis_size(axis)
    place = lax.axis_index(axis)
    chunks = part.reshape(part.shape[0], count, part.shape[1] // count).transpose(1, 0, 2)
    total = lax.dynamic_index_in_dim(chunks, place, 0, False).astype(jnp.float32)
    for step in range(1, count):
        piece = lax.dynamic_index_in_dim(chunks, (place - step) % count, 0, False)
        pairs = [(source, (source - step) % count) for source in range(count)]
        total = total + lax.ppermute(piece, axis, pairs).astype(jnp.float32)
    return total


def per_device(
    events,
    ssm_input,
    gate_input,
    grad_out,
    shared_b,
    shared_c,
    log_decay,
    entry_state,
    w_gate,
    w_value,
    w_shared,
):
    partials = ssd_partials(
        ssm_input, gate_input, grad_out, shared_b, shared_c, log_decay, entry_state[0], SPAN
    )
    block_sum = partials[9]
    block_log = partials[10]
    incoming = suffix_scan((jnp.exp(block_log), block_sum))
    grad_z, grad_x, grad_bc_part = finish_block(partials, incoming)
    grad_bc = summed_over(grad_bc_part, HEAD, 1).astype(jnp.bfloat16)
    input_part = (
        times_rows(grad_z, w_gate) + times_rows(grad_x, w_value) + times_rows(grad_bc, w_shared)
    )
    grad_input = spread_sum(input_part.astype(jnp.bfloat16), HEAD).astype(jnp.bfloat16)
    norm_scale = 1.0 / math.sqrt(events.shape[0] * lax.axis_size(CTX))
    head_cols = grad_z.shape[1]
    projected = jnp.concatenate([grad_z, grad_x, grad_bc], axis=1)
    rows = row_term(events, projected, norm_scale)
    sizes = [lax.axis_size(name) for name in CTX]
    rows = rows.reshape(*sizes, rows.shape[0] // math.prod(sizes), rows.shape[1])
    for level in reversed(range(len(CTX))):
        if level == 0:
            rows, grad_input = lax.optimization_barrier((rows, grad_input))
        rows = summed_over(rows.astype(jnp.bfloat16), CTX[level], level)
    reduced = rows.reshape(rows.shape[-2], rows.shape[-1])
    grad_w_gate = reduced[:, :head_cols]
    grad_w_value = reduced[:, head_cols : 2 * head_cols]
    grad_w_shared = reduced[:, 2 * head_cols :]
    return (grad_input, grad_w_gate, grad_w_value, grad_w_shared)


CTX = ("z", "y_lo", "core")
HEAD = ("y_hi", "x")


def solution(mesh):
    ctx_size, head_size = mesh.devices.shape
    z_size = ctx_size // 4
    fine = jax.sharding.Mesh(
        mesh.devices.reshape(z_size, 2, 2, 2, head_size // 2),
        CTX + HEAD,
    )
    rows = P(CTX, None)
    both = P(CTX, HEAD)
    placed = (
        rows,
        both,
        both,
        both,
        rows,
        rows,
        P(HEAD, CTX),
        P(CTX, HEAD, None, None),
        P(None, HEAD),
        P(None, HEAD),
        P(None, HEAD),
    )
    return jax.shard_map(
        per_device,
        mesh=fine,
        in_specs=placed,
        out_specs=(both, both, both, both),
        check_vma=False,
    )
```

```python
import math

import jax
import jax.numpy as jnp
from jax import lax
from jax.sharding import PartitionSpec as P

SPAN = 256


highest = lax.Precision.HIGHEST


def join(near, far):
    return (near[0] * far[0], near[1] + near[0][..., None, None] * far[1])


def pick(flag, first, second):
    return jax.tree.map(lambda a, b: jnp.where(flag, a, b), first, second)


def swap(tree, axis):
    return jax.tree.map(lambda a: lax.ppermute(a, axis, [(0, 1), (1, 0)]), tree)


def shift(tree, axis, step):
    pairs = [(source, source - step) for source in range(step, lax.axis_size(axis))]
    return jax.tree.map(lambda a: lax.ppermute(a, axis, pairs), tree)


def suffix_scan(part):
    z_axis, pair_axis, core_axis = CTX
    core = lax.axis_index(core_axis)
    pair = lax.axis_index(pair_axis)
    plane = pair * 2 + core
    identity = jax.tree.map(lambda a: jnp.zeros_like(a) + jnp.asarray(1.0 if a.ndim == 1 else 0.0, a.dtype), part)
    other = swap(part, core_axis)
    pair_total = pick(core == 0, join(part, other), join(other, part))
    other_pair = swap(pair_total, pair_axis)
    total = pick(pair == 0, join(pair_total, other_pair), join(other_pair, pair_total))
    within = join(pick(core == 0, other, identity), pick(pair == 0, other_pair, identity))
    head = (
        lax.dynamic_index_in_dim(total[0], plane, 0, False),
        lax.dynamic_index_in_dim(total[1], plane, 0, False),
    )
    one = (jnp.ones_like(head[0]), jnp.zeros_like(head[1]))
    z = lax.axis_index(z_axis)
    count = lax.axis_size(z_axis)
    near = pick(z + 1 < count, shift(head, z_axis, 1), one)
    far = pick(z + 2 < count, shift(head, z_axis, 2), one)
    later = join(near, far)
    step = 2
    while step < count:
        later = pick(z + step < count, join(later, shift(later, z_axis, step)), later)
        step *= 2
    mine = later[1]
    theirs = swap(mine, core_axis)
    two = jnp.where(core == 0, jnp.stack([mine, theirs]), jnp.stack([theirs, mine]))
    two_other = swap(two, pair_axis)
    four = jnp.where(pair == 0, jnp.concatenate([two, two_other]), jnp.concatenate([two_other, two]))
    return within[1] + within[0][:, None, None] * four


def ssd_partials(ssm_input, gate_input, grad_out, shared_b, shared_c, log_decay, entry, block_len):
    head_count, length = log_decay.shape
    head_width = ssm_input.shape[1] // head_count
    span_count = length // block_len
    values_f = ssm_input.astype(jnp.float32).reshape(span_count, block_len, head_count, head_width)
    gates_f = gate_input.astype(jnp.float32).reshape(span_count, block_len, head_count, head_width)
    grad_f = grad_out.astype(jnp.float32).reshape(span_count, block_len, head_count, head_width)
    shared_bf = shared_b.astype(jnp.float32).reshape(span_count, block_len, shared_b.shape[1])
    shared_cf = shared_c.astype(jnp.float32).reshape(span_count, block_len, shared_c.shape[1])
    cumlog = jnp.cumsum(log_decay.reshape(head_count, span_count, block_len), axis=2)
    totals = cumlog[:, :, -1]
    causal = jnp.arange(block_len)[:, None] >= jnp.arange(block_len)[None, :]
    spread = cumlog[:, :, :, None] - cumlog[:, :, None, :]
    decay_mat = jnp.where(causal, jnp.exp(jnp.minimum(spread, 0.0)), 0.0)
    shared_c_blocks = shared_c.reshape(span_count, block_len, shared_c.shape[1])
    shared_b_blocks = shared_b.reshape(span_count, block_len, shared_b.shape[1])
    scores = jnp.einsum(
        "ktn,ksn->kts", shared_c_blocks, shared_b_blocks, preferred_element_type=jnp.float32
    )
    weighted = decay_mat * scores[None]
    to_end = jnp.exp(totals[:, :, None] - cumlog).transpose(1, 2, 0)
    from_start = jnp.exp(cumlog).transpose(1, 2, 0)
    scaled_x = values_f * to_end[..., None]
    local_states = jnp.einsum("ksn,kshp->khnp", shared_bf, scaled_x, precision=highest)
    span_decay = jnp.exp(totals).T

    def forward_step(running, inputs):
        decay_k, local_k = inputs
        return (decay_k[:, None, None] * running + local_k, running)

    _, entries = lax.scan(forward_step, entry, (span_decay, local_states))
    ssm_out = jnp.einsum("hkts,kshp->kthp", weighted, values_f, precision=highest)
    ssm_out = ssm_out + from_start[..., None] * jnp.einsum(
        "ktn,khnp->kthp", shared_cf, entries, precision=highest
    )
    gate_sig = jax.nn.sigmoid(gates_f)
    grad_y = grad_f * gates_f * gate_sig
    grad_z = grad_f * ssm_out * gate_sig * (1.0 + gates_f * (1.0 - gate_sig))
    products = decay_mat * jnp.einsum("kthp,kshp->hkts", grad_y, values_f, precision=highest)
    scaled_dy = grad_y * from_start[..., None]
    grad_c = jnp.einsum("hkts,ksn->ktn", products, shared_bf, precision=highest)
    grad_c = grad_c + jnp.einsum("kthp,khnp->ktn", scaled_dy, entries, precision=highest)
    grad_b = jnp.einsum("hkst,ksn->ktn", products, shared_cf, precision=highest)
    grad_x = jnp.einsum("hkst,kshp->kthp", weighted, grad_y, precision=highest)
    block_terms = jnp.einsum("ksn,kshp->khnp", shared_cf, scaled_dy, precision=highest)

    def backward_step(running, inputs):
        decay_k, term_k = inputs
        return (term_k + decay_k[:, None, None] * running, running)

    block_sum, later_sums = lax.scan(
        backward_step, jnp.zeros_like(entry), (span_decay, block_terms), reverse=True
    )
    block_log = jnp.sum(totals, axis=1)
    suffix = block_log[None, :] - jnp.cumsum(totals, axis=1).T
    grad_z_out = grad_z.reshape(length, head_count * head_width).astype(jnp.bfloat16)
    return (
        grad_z_out,
        grad_x,
        grad_b,
        grad_c,
        later_sums,
        suffix,
        to_end,
        scaled_x,
        shared_bf,
        block_sum,
        block_log,
    )


def finish_block(partials, incoming):
    (
        grad_z_out,
        grad_x,
        grad_b,
        grad_c,
        later_sums,
        suffix,
        to_end,
        scaled_x,
        shared_bf,
        block_sum,
        block_log,
    ) = partials
    carried = later_sums + jnp.exp(suffix)[:, :, None, None] * incoming[None]
    grad_x = grad_x + to_end[..., None] * jnp.einsum(
        "ktn,khnp->kthp", shared_bf, carried, precision=highest
    )
    grad_b = grad_b + jnp.einsum("kthp,khnp->ktn", scaled_x, carried, precision=highest)
    length = grad_z_out.shape[0]
    grad_x_out = grad_x.reshape(length, grad_z_out.shape[1]).astype(jnp.bfloat16)
    grad_bc = jnp.concatenate([grad_b.reshape(length, -1), grad_c.reshape(length, -1)], axis=1)
    return (grad_z_out, grad_x_out, grad_bc)


def times_rows(left, weights):
    return lax.dot_general(
        left, weights, (((1,), (1,)), ((), ())), preferred_element_type=jnp.float32
    )


def row_term(events, projected, norm_scale):
    return (
        lax.dot_general(
            events, projected, (((0,), (0,)), ((), ())), preferred_element_type=jnp.float32
        )
        * norm_scale
    )


def summed_over(part, axis, split):
    gathered = lax.all_to_all(part, axis, split, split, tiled=True)
    shape = gathered.shape
    pieces = shape[:split] + (lax.axis_size(axis), shape[split] // lax.axis_size(axis)) + shape[split + 1 :]
    return jnp.sum(gathered.astype(jnp.float32).reshape(pieces), axis=split)


def spread_sum(part, axis):
    count = lax.axis_size(axis)
    place = lax.axis_index(axis)
    chunks = part.reshape(part.shape[0], count, part.shape[1] // count).transpose(1, 0, 2)
    total = lax.dynamic_index_in_dim(chunks, place, 0, False).astype(jnp.float32)
    for step in range(1, count):
        piece = lax.dynamic_index_in_dim(chunks, (place - step) % count, 0, False)
        pairs = [(source, (source - step) % count) for source in range(count)]
        total = total + lax.ppermute(piece, axis, pairs).astype(jnp.float32)
    return total


def per_device(
    events,
    ssm_input,
    gate_input,
    grad_out,
    shared_b,
    shared_c,
    log_decay,
    entry_state,
    w_gate,
    w_value,
    w_shared,
):
    partials = ssd_partials(
        ssm_input, gate_input, grad_out, shared_b, shared_c, log_decay, entry_state[0], SPAN
    )
    block_sum = partials[9]
    block_log = partials[10]
    incoming = suffix_scan((jnp.exp(block_log), block_sum))
    grad_z, grad_x, grad_bc_part = finish_block(partials, incoming)
    grad_bc = summed_over(grad_bc_part.astype(jnp.bfloat16), HEAD, 1).astype(jnp.bfloat16)
    input_part = (
        times_rows(grad_z, w_gate) + times_rows(grad_x, w_value) + times_rows(grad_bc, w_shared)
    )
    grad_input = spread_sum(input_part.astype(jnp.bfloat16), HEAD).astype(jnp.bfloat16)
    norm_scale = 1.0 / math.sqrt(events.shape[0] * lax.axis_size(CTX))
    head_cols = grad_z.shape[1]
    projected = jnp.concatenate([grad_z, grad_x, grad_bc], axis=1)
    rows = row_term(events, projected, norm_scale)
    sizes = [lax.axis_size(name) for name in CTX]
    rows = rows.reshape(*sizes, rows.shape[0] // math.prod(sizes), rows.shape[1])
    for level in reversed(range(len(CTX))):
        rows = summed_over(rows.astype(jnp.bfloat16), CTX[level], level)
    reduced = rows.reshape(rows.shape[-2], rows.shape[-1])
    grad_w_gate = reduced[:, :head_cols]
    grad_w_value = reduced[:, head_cols : 2 * head_cols]
    grad_w_shared = reduced[:, 2 * head_cols :]
    return (grad_input, grad_w_gate, grad_w_value, grad_w_shared)


CTX = ("z", "y_lo", "core")
HEAD = ("y_hi", "x")


def solution(mesh):
    ctx_size, head_size = mesh.devices.shape
    z_size = ctx_size // 4
    fine = jax.sharding.Mesh(
        mesh.devices.reshape(z_size, 2, 2, 2, head_size // 2),
        CTX + HEAD,
    )
    rows = P(CTX, None)
    both = P(CTX, HEAD)
    placed = (
        rows,
        both,
        both,
        both,
        rows,
        rows,
        P(HEAD, CTX),
        P(CTX, HEAD, None, None),
        P(None, HEAD),
        P(None, HEAD),
        P(None, HEAD),
    )
    return jax.shard_map(
        per_device,
        mesh=fine,
        in_specs=placed,
        out_specs=(both, both, both, both),
        check_vma=False,
    )
```

```python
import math

import jax
import jax.numpy as jnp
from jax import lax
from jax.sharding import PartitionSpec as P

SPAN = 256


highest = lax.Precision.HIGHEST


def join(near, far):
    return (near[0] * far[0], near[1] + near[0][..., None, None] * far[1])


def pick(flag, first, second):
    return jax.tree.map(lambda a, b: jnp.where(flag, a, b), first, second)


def swap(tree, axis):
    return jax.tree.map(lambda a: lax.ppermute(a, axis, [(0, 1), (1, 0)]), tree)


def shift(tree, axis, step):
    pairs = [(source, source - step) for source in range(step, lax.axis_size(axis))]
    return jax.tree.map(lambda a: lax.ppermute(a, axis, pairs), tree)


def suffix_scan(part):
    z_axis, pair_axis, core_axis = CTX
    core = lax.axis_index(core_axis)
    pair = lax.axis_index(pair_axis)
    plane = pair * 2 + core
    identity = jax.tree.map(lambda a: jnp.zeros_like(a) + jnp.asarray(1.0 if a.ndim == 1 else 0.0, a.dtype), part)
    other = swap(part, core_axis)
    pair_total = pick(core == 0, join(part, other), join(other, part))
    other_pair = swap(pair_total, pair_axis)
    total = pick(pair == 0, join(pair_total, other_pair), join(other_pair, pair_total))
    within = join(pick(core == 0, other, identity), pick(pair == 0, other_pair, identity))
    head = (
        lax.dynamic_index_in_dim(total[0], plane, 0, False),
        lax.dynamic_index_in_dim(total[1], plane, 0, False),
    )
    one = (jnp.ones_like(head[0]), jnp.zeros_like(head[1]))
    z = lax.axis_index(z_axis)
    count = lax.axis_size(z_axis)
    near = pick(z + 1 < count, shift(head, z_axis, 1), one)
    far = pick(z + 2 < count, shift(head, z_axis, 2), one)
    later = join(near, far)
    step = 2
    while step < count:
        later = pick(z + step < count, join(later, shift(later, z_axis, step)), later)
        step *= 2
    mine = later[1]
    theirs = swap(mine, core_axis)
    two = jnp.where(core == 0, jnp.stack([mine, theirs]), jnp.stack([theirs, mine]))
    two_other = swap(two, pair_axis)
    four = jnp.where(pair == 0, jnp.concatenate([two, two_other]), jnp.concatenate([two_other, two]))
    return within[1] + within[0][:, None, None] * four


def ssd_partials(ssm_input, gate_input, grad_out, shared_b, shared_c, log_decay, entry, block_len):
    head_count, length = log_decay.shape
    head_width = ssm_input.shape[1] // head_count
    span_count = length // block_len
    values_f = ssm_input.astype(jnp.float32).reshape(span_count, block_len, head_count, head_width)
    gates_f = gate_input.astype(jnp.float32).reshape(span_count, block_len, head_count, head_width)
    grad_f = grad_out.astype(jnp.float32).reshape(span_count, block_len, head_count, head_width)
    shared_bf = shared_b.astype(jnp.float32).reshape(span_count, block_len, shared_b.shape[1])
    shared_cf = shared_c.astype(jnp.float32).reshape(span_count, block_len, shared_c.shape[1])
    cumlog = jnp.cumsum(log_decay.reshape(head_count, span_count, block_len), axis=2)
    totals = cumlog[:, :, -1]
    causal = jnp.arange(block_len)[:, None] >= jnp.arange(block_len)[None, :]
    spread = cumlog[:, :, :, None] - cumlog[:, :, None, :]
    decay_mat = jnp.where(causal, jnp.exp(jnp.minimum(spread, 0.0)), 0.0)
    shared_c_blocks = shared_c.reshape(span_count, block_len, shared_c.shape[1])
    shared_b_blocks = shared_b.reshape(span_count, block_len, shared_b.shape[1])
    scores = jnp.einsum(
        "ktn,ksn->kts", shared_c_blocks, shared_b_blocks, preferred_element_type=jnp.float32
    )
    weighted = decay_mat * scores[None]
    to_end = jnp.exp(totals[:, :, None] - cumlog).transpose(1, 2, 0)
    from_start = jnp.exp(cumlog).transpose(1, 2, 0)
    scaled_x = values_f * to_end[..., None]
    local_states = jnp.einsum("ksn,kshp->khnp", shared_bf, scaled_x, precision=highest)
    span_decay = jnp.exp(totals).T

    def forward_step(running, inputs):
        decay_k, local_k = inputs
        return (decay_k[:, None, None] * running + local_k, running)

    _, entries = lax.scan(forward_step, entry, (span_decay, local_states))
    ssm_out = jnp.einsum("hkts,kshp->kthp", weighted, values_f, precision=highest)
    ssm_out = ssm_out + from_start[..., None] * jnp.einsum(
        "ktn,khnp->kthp", shared_cf, entries, precision=highest
    )
    gate_sig = jax.nn.sigmoid(gates_f)
    grad_y = grad_f * gates_f * gate_sig
    grad_z = grad_f * ssm_out * gate_sig * (1.0 + gates_f * (1.0 - gate_sig))
    products = decay_mat * jnp.einsum("kthp,kshp->hkts", grad_y, values_f, precision=highest)
    scaled_dy = grad_y * from_start[..., None]
    grad_c = jnp.einsum("hkts,ksn->ktn", products, shared_bf, precision=highest)
    grad_c = grad_c + jnp.einsum("kthp,khnp->ktn", scaled_dy, entries, precision=highest)
    grad_b = jnp.einsum("hkst,ksn->ktn", products, shared_cf, precision=highest)
    grad_x = jnp.einsum("hkst,kshp->kthp", weighted, grad_y, precision=highest)
    block_terms = jnp.einsum("ksn,kshp->khnp", shared_cf, scaled_dy, precision=highest)

    def backward_step(running, inputs):
        decay_k, term_k = inputs
        return (term_k + decay_k[:, None, None] * running, running)

    block_sum, later_sums = lax.scan(
        backward_step, jnp.zeros_like(entry), (span_decay, block_terms), reverse=True
    )
    block_log = jnp.sum(totals, axis=1)
    suffix = block_log[None, :] - jnp.cumsum(totals, axis=1).T
    grad_z_out = grad_z.reshape(length, head_count * head_width).astype(jnp.bfloat16)
    return (
        grad_z_out,
        grad_x,
        grad_b,
        grad_c,
        later_sums,
        suffix,
        to_end,
        scaled_x,
        shared_bf,
        block_sum,
        block_log,
    )


def finish_block(partials, incoming):
    (
        grad_z_out,
        grad_x,
        grad_b,
        grad_c,
        later_sums,
        suffix,
        to_end,
        scaled_x,
        shared_bf,
        block_sum,
        block_log,
    ) = partials
    carried = later_sums + jnp.exp(suffix)[:, :, None, None] * incoming[None]
    grad_x = grad_x + to_end[..., None] * jnp.einsum(
        "ktn,khnp->kthp", shared_bf, carried, precision=highest
    )
    grad_b = grad_b + jnp.einsum("kthp,khnp->ktn", scaled_x, carried, precision=highest)
    length = grad_z_out.shape[0]
    grad_x_out = grad_x.reshape(length, grad_z_out.shape[1]).astype(jnp.bfloat16)
    grad_bc = jnp.concatenate([grad_b.reshape(length, -1), grad_c.reshape(length, -1)], axis=1)
    return (grad_z_out, grad_x_out, grad_bc)


def times_rows(left, weights):
    return lax.dot_general(
        left, weights, (((1,), (1,)), ((), ())), preferred_element_type=jnp.float32
    )


def row_term(events, projected, norm_scale):
    return (
        lax.dot_general(
            events, projected, (((0,), (0,)), ((), ())), preferred_element_type=jnp.float32
        )
        * norm_scale
    )


def summed_over(part, axis, split):
    gathered = lax.all_to_all(part, axis, split, split, tiled=True)
    shape = gathered.shape
    pieces = shape[:split] + (lax.axis_size(axis), shape[split] // lax.axis_size(axis)) + shape[split + 1 :]
    return jnp.sum(gathered.astype(jnp.float32).reshape(pieces), axis=split)


def spread_sum(part, axis):
    count = lax.axis_size(axis)
    place = lax.axis_index(axis)
    chunks = part.reshape(part.shape[0], count, part.shape[1] // count).transpose(1, 0, 2)
    total = lax.dynamic_index_in_dim(chunks, place, 0, False).astype(jnp.float32)
    for step in range(1, count):
        piece = lax.dynamic_index_in_dim(chunks, (place - step) % count, 0, False)
        pairs = [(source, (source - step) % count) for source in range(count)]
        total = total + lax.ppermute(piece, axis, pairs).astype(jnp.float32)
    return total


def swap_sum(rows, axis, dim):
    place = lax.axis_index(axis)
    own = lax.dynamic_index_in_dim(rows, place, dim, True)
    other = lax.dynamic_index_in_dim(rows, 1 - place, dim, True)
    return own + swap(other.astype(jnp.bfloat16), axis).astype(jnp.float32)


def per_device(
    events,
    ssm_input,
    gate_input,
    grad_out,
    shared_b,
    shared_c,
    log_decay,
    entry_state,
    w_gate,
    w_value,
    w_shared,
):
    partials = ssd_partials(
        ssm_input, gate_input, grad_out, shared_b, shared_c, log_decay, entry_state[0], SPAN
    )
    block_sum = partials[9]
    block_log = partials[10]
    incoming = suffix_scan((jnp.exp(block_log), block_sum))
    grad_z, grad_x, grad_bc_part = finish_block(partials, incoming)
    grad_bc = summed_over(grad_bc_part.astype(jnp.bfloat16), HEAD, 1).astype(jnp.bfloat16)
    input_part = (
        times_rows(grad_z, w_gate) + times_rows(grad_x, w_value) + times_rows(grad_bc, w_shared)
    )
    grad_input = spread_sum(input_part.astype(jnp.bfloat16), HEAD).astype(jnp.bfloat16)
    norm_scale = 1.0 / math.sqrt(events.shape[0] * lax.axis_size(CTX))
    head_cols = grad_z.shape[1]
    projected = jnp.concatenate([grad_z, grad_x, grad_bc], axis=1)
    rows = row_term(events, projected, norm_scale)
    sizes = [lax.axis_size(name) for name in CTX]
    rows = rows.reshape(*sizes, rows.shape[0] // math.prod(sizes), rows.shape[1])
    for level in reversed(range(len(CTX))):
        if level == len(CTX) - 1:
            rows = swap_sum(rows, CTX[level], level)
        else:
            rows = summed_over(rows.astype(jnp.bfloat16), CTX[level], level)
    reduced = rows.reshape(rows.shape[-2], rows.shape[-1])
    grad_w_gate = reduced[:, :head_cols]
    grad_w_value = reduced[:, head_cols : 2 * head_cols]
    grad_w_shared = reduced[:, 2 * head_cols :]
    return (grad_input, grad_w_gate, grad_w_value, grad_w_shared)


CTX = ("z", "y_lo", "core")
HEAD = ("y_hi", "x")


def solution(mesh):
    ctx_size, head_size = mesh.devices.shape
    z_size = ctx_size // 4
    fine = jax.sharding.Mesh(
        mesh.devices.reshape(z_size, 2, 2, 2, head_size // 2),
        CTX + HEAD,
    )
    rows = P(CTX, None)
    both = P(CTX, HEAD)
    placed = (
        rows,
        both,
        both,
        both,
        rows,
        rows,
        P(HEAD, CTX),
        P(CTX, HEAD, None, None),
        P(None, HEAD),
        P(None, HEAD),
        P(None, HEAD),
    )
    return jax.shard_map(
        per_device,
        mesh=fine,
        in_specs=placed,
        out_specs=(both, both, both, both),
        check_vma=False,
    )
```

```python
import math

import jax
import jax.numpy as jnp
from jax import lax
from jax.sharding import PartitionSpec as P

SPAN = 256


highest = lax.Precision.HIGHEST


def join(near, far):
    return (near[0] * far[0], near[1] + near[0][..., None, None] * far[1])


def pick(flag, first, second):
    return jax.tree.map(lambda a, b: jnp.where(flag, a, b), first, second)


def swap(tree, axis):
    return jax.tree.map(lambda a: lax.ppermute(a, axis, [(0, 1), (1, 0)]), tree)


def shift(tree, axis, step):
    pairs = [(source, source - step) for source in range(step, lax.axis_size(axis))]
    return jax.tree.map(lambda a: lax.ppermute(a, axis, pairs), tree)


def suffix_scan(part):
    z_axis, pair_axis, core_axis = CTX
    core = lax.axis_index(core_axis)
    pair = lax.axis_index(pair_axis)
    plane = pair * 2 + core
    identity = jax.tree.map(lambda a: jnp.zeros_like(a) + jnp.asarray(1.0 if a.ndim == 1 else 0.0, a.dtype), part)
    other = swap(part, core_axis)
    pair_total = pick(core == 0, join(part, other), join(other, part))
    other_pair = swap(pair_total, pair_axis)
    total = pick(pair == 0, join(pair_total, other_pair), join(other_pair, pair_total))
    within = join(pick(core == 0, other, identity), pick(pair == 0, other_pair, identity))
    head = (
        lax.dynamic_index_in_dim(total[0], plane, 0, False),
        lax.dynamic_index_in_dim(total[1], plane, 0, False),
    )
    one = (jnp.ones_like(head[0]), jnp.zeros_like(head[1]))
    z = lax.axis_index(z_axis)
    count = lax.axis_size(z_axis)
    near = pick(z + 1 < count, shift(head, z_axis, 1), one)
    far = pick(z + 2 < count, shift(head, z_axis, 2), one)
    later = join(near, far)
    step = 2
    while step < count:
        later = pick(z + step < count, join(later, shift(later, z_axis, step)), later)
        step *= 2
    mine = later[1]
    theirs = swap(mine, core_axis)
    two = jnp.where(core == 0, jnp.stack([mine, theirs]), jnp.stack([theirs, mine]))
    two_other = swap(two, pair_axis)
    four = jnp.where(pair == 0, jnp.concatenate([two, two_other]), jnp.concatenate([two_other, two]))
    return within[1] + within[0][:, None, None] * four


def ssd_partials(ssm_input, gate_input, grad_out, shared_b, shared_c, log_decay, entry, block_len):
    head_count, length = log_decay.shape
    head_width = ssm_input.shape[1] // head_count
    span_count = length // block_len
    values_f = ssm_input.astype(jnp.float32).reshape(span_count, block_len, head_count, head_width)
    gates_f = gate_input.astype(jnp.float32).reshape(span_count, block_len, head_count, head_width)
    grad_f = grad_out.astype(jnp.float32).reshape(span_count, block_len, head_count, head_width)
    shared_bf = shared_b.astype(jnp.float32).reshape(span_count, block_len, shared_b.shape[1])
    shared_cf = shared_c.astype(jnp.float32).reshape(span_count, block_len, shared_c.shape[1])
    cumlog = jnp.cumsum(log_decay.reshape(head_count, span_count, block_len), axis=2)
    totals = cumlog[:, :, -1]
    causal = jnp.arange(block_len)[:, None] >= jnp.arange(block_len)[None, :]
    spread = cumlog[:, :, :, None] - cumlog[:, :, None, :]
    decay_mat = jnp.where(causal, jnp.exp(jnp.minimum(spread, 0.0)), 0.0)
    shared_c_blocks = shared_c.reshape(span_count, block_len, shared_c.shape[1])
    shared_b_blocks = shared_b.reshape(span_count, block_len, shared_b.shape[1])
    scores = jnp.einsum(
        "ktn,ksn->kts", shared_c_blocks, shared_b_blocks, preferred_element_type=jnp.float32
    )
    weighted = decay_mat * scores[None]
    to_end = jnp.exp(totals[:, :, None] - cumlog).transpose(1, 2, 0)
    from_start = jnp.exp(cumlog).transpose(1, 2, 0)
    scaled_x = values_f * to_end[..., None]
    local_states = jnp.einsum("ksn,kshp->khnp", shared_bf, scaled_x, precision=highest)
    span_decay = jnp.exp(totals).T

    def forward_step(running, inputs):
        decay_k, local_k = inputs
        return (decay_k[:, None, None] * running + local_k, running)

    _, entries = lax.scan(forward_step, entry, (span_decay, local_states))
    ssm_out = jnp.einsum("hkts,kshp->kthp", weighted, values_f, precision=highest)
    ssm_out = ssm_out + from_start[..., None] * jnp.einsum(
        "ktn,khnp->kthp", shared_cf, entries, precision=highest
    )
    gate_sig = jax.nn.sigmoid(gates_f)
    grad_y = grad_f * gates_f * gate_sig
    grad_z = grad_f * ssm_out * gate_sig * (1.0 + gates_f * (1.0 - gate_sig))
    products = decay_mat * jnp.einsum("kthp,kshp->hkts", grad_y, values_f, precision=highest)
    scaled_dy = grad_y * from_start[..., None]
    grad_c = jnp.einsum("hkts,ksn->ktn", products, shared_bf, precision=highest)
    grad_c = grad_c + jnp.einsum("kthp,khnp->ktn", scaled_dy, entries, precision=highest)
    grad_b = jnp.einsum("hkst,ksn->ktn", products, shared_cf, precision=highest)
    grad_x = jnp.einsum("hkst,kshp->kthp", weighted, grad_y, precision=highest)
    block_terms = jnp.einsum("ksn,kshp->khnp", shared_cf, scaled_dy, precision=highest)

    def backward_step(running, inputs):
        decay_k, term_k = inputs
        return (term_k + decay_k[:, None, None] * running, running)

    block_sum, later_sums = lax.scan(
        backward_step, jnp.zeros_like(entry), (span_decay, block_terms), reverse=True
    )
    block_log = jnp.sum(totals, axis=1)
    suffix = block_log[None, :] - jnp.cumsum(totals, axis=1).T
    grad_z_out = grad_z.reshape(length, head_count * head_width).astype(jnp.bfloat16)
    return (
        grad_z_out,
        grad_x,
        grad_b,
        grad_c,
        later_sums,
        suffix,
        to_end,
        scaled_x,
        shared_bf,
        block_sum,
        block_log,
    )


def finish_block(partials, incoming):
    (
        grad_z_out,
        grad_x,
        grad_b,
        grad_c,
        later_sums,
        suffix,
        to_end,
        scaled_x,
        shared_bf,
        block_sum,
        block_log,
    ) = partials
    carried = later_sums + jnp.exp(suffix)[:, :, None, None] * incoming[None]
    grad_x = grad_x + to_end[..., None] * jnp.einsum(
        "ktn,khnp->kthp", shared_bf, carried, precision=highest
    )
    grad_b = grad_b + jnp.einsum("kthp,khnp->ktn", scaled_x, carried, precision=highest)
    length = grad_z_out.shape[0]
    grad_x_out = grad_x.reshape(length, grad_z_out.shape[1]).astype(jnp.bfloat16)
    grad_bc = jnp.concatenate([grad_b.reshape(length, -1), grad_c.reshape(length, -1)], axis=1)
    return (grad_z_out, grad_x_out, grad_bc)


def times_rows(left, weights):
    return lax.dot_general(
        left, weights, (((1,), (1,)), ((), ())), preferred_element_type=jnp.float32
    )


def row_term(events, projected, norm_scale):
    return (
        lax.dot_general(
            events, projected, (((0,), (0,)), ((), ())), preferred_element_type=jnp.float32
        )
        * norm_scale
    )


def summed_over(part, axis, split):
    gathered = lax.all_to_all(part, axis, split, split, tiled=True)
    shape = gathered.shape
    pieces = shape[:split] + (lax.axis_size(axis), shape[split] // lax.axis_size(axis)) + shape[split + 1 :]
    return jnp.sum(gathered.astype(jnp.float32).reshape(pieces), axis=split)


def spread_sum(part, axis):
    count = lax.axis_size(axis)
    place = lax.axis_index(axis)
    chunks = part.reshape(part.shape[0], count, part.shape[1] // count).transpose(1, 0, 2)
    total = lax.dynamic_index_in_dim(chunks, place, 0, False).astype(jnp.float32)
    for step in range(1, count):
        piece = lax.dynamic_index_in_dim(chunks, (place - step) % count, 0, False)
        pairs = [(source, (source - step) % count) for source in range(count)]
        total = total + lax.ppermute(piece, axis, pairs).astype(jnp.float32)
    return total


def per_device(
    events,
    ssm_input,
    gate_input,
    grad_out,
    shared_b,
    shared_c,
    log_decay,
    entry_state,
    w_gate,
    w_value,
    w_shared,
):
    partials = ssd_partials(
        ssm_input, gate_input, grad_out, shared_b, shared_c, log_decay, entry_state[0], SPAN
    )
    block_sum = partials[9]
    block_log = partials[10]
    incoming = suffix_scan((jnp.exp(block_log), block_sum))
    grad_z, grad_x, grad_bc_part = finish_block(partials, incoming)
    grad_bc = summed_over(grad_bc_part.astype(jnp.bfloat16), HEAD, 1).astype(jnp.bfloat16)
    input_part = (
        times_rows(grad_z, w_gate) + times_rows(grad_x, w_value) + times_rows(grad_bc, w_shared)
    )
    grad_input = spread_sum(input_part.astype(jnp.bfloat16), HEAD).astype(jnp.bfloat16)
    norm_scale = 1.0 / math.sqrt(events.shape[0] * lax.axis_size(CTX))
    head_cols = grad_z.shape[1]
    projected = jnp.concatenate([grad_z, grad_x, grad_bc], axis=1)
    rows = row_term(events, projected, norm_scale)
    sizes = [lax.axis_size(name) for name in CTX]
    rows = rows.reshape(*sizes, rows.shape[0] // math.prod(sizes), rows.shape[1])
    for level in reversed(range(1, len(CTX))):
        rows = summed_over(rows.astype(jnp.bfloat16), CTX[level], level)
    flat = rows.reshape(rows.shape[0], -1).astype(jnp.bfloat16)
    rows = summed_over(flat, CTX[0], 0).reshape(1, 1, 1, rows.shape[-2], rows.shape[-1])
    reduced = rows.reshape(rows.shape[-2], rows.shape[-1])
    grad_w_gate = reduced[:, :head_cols]
    grad_w_value = reduced[:, head_cols : 2 * head_cols]
    grad_w_shared = reduced[:, 2 * head_cols :]
    return (grad_input, grad_w_gate, grad_w_value, grad_w_shared)


CTX = ("z", "y_lo", "core")
HEAD = ("y_hi", "x")


def solution(mesh):
    ctx_size, head_size = mesh.devices.shape
    z_size = ctx_size // 4
    fine = jax.sharding.Mesh(
        mesh.devices.reshape(z_size, 2, 2, 2, head_size // 2),
        CTX + HEAD,
    )
    rows = P(CTX, None)
    both = P(CTX, HEAD)
    placed = (
        rows,
        both,
        both,
        both,
        rows,
        rows,
        P(HEAD, CTX),
        P(CTX, HEAD, None, None),
        P(None, HEAD),
        P(None, HEAD),
        P(None, HEAD),
    )
    return jax.shard_map(
        per_device,
        mesh=fine,
        in_specs=placed,
        out_specs=(both, both, both, both),
        check_vma=False,
    )
```
